512 devices in a mesh: dp: 4 (over x), seq: 16 (over z, core), head: 8 (over y).
Axes of the slice: x: 4, y: 8, z: 8, core: 2. Of those that a mesh axis runs over, the one named last changes fastest.
Arguments:
- doc_ids: int32 [16384], P(('dp', 'seq')), parts along dimension 0, may hold values from 0 to 7, never falling along the last dimension, each value on 1 to 2048 neighbouring positions
- light_q: bfloat16 [16384, 4096], P(('dp', 'seq'), 'head'), parts along dimension 0, may hold values from -0.59765625 to 0.59765625
- light_k: bfloat16 [16384, 4096], P(('dp', 'seq'), 'head'), parts along dimension 0, may hold values from -0.59765625 to 0.59765625
- light_v: bfloat16 [16384, 4096], P(('dp', 'seq'), 'head'), parts along dimension 0, may hold values from -6 to 6
- light_decay: float32 [32], P('head'), may hold values from 0 to 1
- light_grad_out: bfloat16 [16384, 4096], P(('dp', 'seq'), 'head'), parts along dimension 0, may hold values from -6 to 6
- soft_q: bfloat16 [16384, 4096], P(('dp', 'seq'), 'head'), parts along dimension 0, may hold values from -40 to 40
- soft_k: bfloat16 [16384, 4096], P(('dp', 'seq'), 'head'), parts along dimension 0, may hold values from -40 to 40
- soft_v: bfloat16 [16384, 4096], P(('dp', 'seq'), 'head'), parts along dimension 0, may hold values from -6 to 6
- soft_grad_out: bfloat16 [16384, 4096], P(('dp', 'seq'), 'head'), parts along dimension 0, may hold values from -6 to 6
Outputs:
- lightning_output: bfloat16 [16384, 4096], P(('dp', 'seq'), 'head'), parts along dimension 0
- lightning_query_gradient: bfloat16 [16384, 4096], P(('dp', 'seq'), 'head'), parts along dimension 0
- lightning_key_gradient: bfloat16 [16384, 4096], P(('dp', 'seq'), 'head'), parts along dimension 0
- lightning_value_gradient: bfloat16 [16384, 4096], P(('dp', 'seq'), 'head'), parts along dimension 0
- soft_out: bfloat16 [16384, 4096], P(('dp', 'seq'), 'head'), parts along dimension 0
- soft_dq: bfloat16 [16384, 4096], P(('dp', 'seq'), 'head'), parts along dimension 0
- soft_dk: bfloat16 [16384, 4096], P(('dp', 'seq'), 'head'), parts along dimension 0
- soft_dv: bfloat16 [16384, 4096], P(('dp', 'seq'), 'head'), parts along dimension 0
The draws below stay inside these ranges and needn't reach their ends.
There are 4 independent parts, one for each index of `dp`. The reference program is written for one: setup_inputs(seed, part) draws one part's arguments, and reference() takes and returns one part's arrays. A program takes and returns all parts, laid end to end along the dimension named above; an argument that names none is the same for every part. Nothing has to cross between parts.
Inputs may be any that keep to these rules, and one draw needn't show every extreme that they name: `doc_ids`: document ids never fall along the sequence; each document holds at most 2048 tokens, and one holds exactly that many.
All inputs are finite; a program needn't handle non-finite values.
Results may differ from the reference program's by a relative error of at most 0.02.
Values may be sent and summed in bfloat16 or wider, within the bound.
No kernel may reach another device: no remote copies, remote signals or barrier semaphores. Data moves between devices by JAX's collectives and lax.ppermute only.
A program may use at most 128 MiB of HBM per device.

```python
import math
import jax
import jax.numpy as jnp
import numpy as np
from jax import lax

H = 32
HD = 128
DOCS = 8
TOKENS = 4096


def draw_light_decay(key, part):
    base = jax.random.fold_in(key, 5309)
    slow_flag = jax.random.randint(jax.random.fold_in(base, 1), (H,), 0, 2) == 1
    slow_rate = jnp.exp(jax.random.uniform(jax.random.fold_in(base, 2), (H,), jnp.float32, math.log(1.0 / (16.0 * TOKENS)), math.log(1.0 / (4.0 * TOKENS))))
    fast_rate = jnp.exp(jax.random.uniform(jax.random.fold_in(base, 3), (H,), jnp.float32, math.log(1.0 / 50.0), math.log(1.0 / 20.0)))
    return jnp.where(slow_flag, slow_rate, fast_rate).astype(jnp.float32)


def soft_pair(key):
    base = jax.random.fold_in(key, 7103)
    query = jax.random.normal(jax.random.fold_in(base, 1), (TOKENS, H, HD), jnp.float32)
    keys = jax.random.normal(jax.random.fold_in(base, 2), (TOKENS, H, HD), jnp.float32)
    return (query.reshape(TOKENS, H * HD), keys.reshape(TOKENS, H * HD))


def draw_soft_q(key, part):
    return soft_pair(key)[0].astype(jnp.bfloat16)


def draw_soft_k(key, part):
    return soft_pair(key)[1].astype(jnp.bfloat16)


def levels(own_key, extent, shards, least, high):
    loudness = 1.0
    for axis_at, blocks in shards:
        draws = jax.random.uniform(jax.random.fold_in(jax.random.fold_in(own_key, 6), axis_at), (blocks,), jnp.float32, least / len(shards), high / len(shards))
        loudness = loudness * jnp.repeat(jnp.exp(draws), extent[axis_at] // blocks).reshape((-1,) + (1,) * (len(extent) - 1 - axis_at))
    return loudness


def split_up(amount, total, reach, lean):
    weights = [(1 << 20) // math.isqrt(standing ** lean) + 1 for standing in range(2, amount + 1)]
    spare, counts = total - reach - (amount - 1), [1] * (amount - 1)
    while spare > 0:
        movable = [i for i in range(amount - 1) if counts[i] < reach]
        whole, left = sum([weights[i] for i in movable]), spare
        for i in movable:
            more = min(reach - counts[i], max(1, left * weights[i] // whole), spare)
            counts[i] = counts[i] + more
            spare = spare - more
    return np.array([reach] + counts)


def ragged(own_key, number_of, total, bound, lean):
    if number_of == 2:
        one = jax.random.randint(own_key, (), max(1, total - bound), min(bound, total - 1) + 1)
        return jnp.stack([one, total - one])
    sizes = jnp.asarray(split_up(number_of, total, bound, lean), jnp.int32)
    twos = (number_of - 1) // 2
    source_of, receiver = sizes[1:1 + 2 * twos:2], sizes[2:2 + 2 * twos:2]
    room = jnp.minimum(source_of - 1, bound - receiver)
    moved = jax.random.randint(jax.random.fold_in(own_key, 1), (twos,), 0, 1 << 20) % (room + 1)
    sizes = sizes.at[1:1 + 2 * twos:2].set(source_of - moved).at[2:2 + 2 * twos:2].set(receiver + moved)
    return sizes[jax.random.permutation(jax.random.fold_in(own_key, 2), number_of)]


def bell_draw(own_key, dims, deviation, limit, split=(), kind=jnp.bfloat16):
    gain = levels(own_key, dims, split, -0.22, 0.18) if split else 1.0
    result = jax.random.normal(own_key, dims, jnp.float32) * deviation * gain
    return jnp.minimum(jnp.maximum(result, -limit), limit).astype(kind)


def setup_inputs(seed: int = 0, part: int = 0) -> dict:
    key_list = jax.random.split(jax.random.key(seed), 11)
    part_splits = jax.random.split(jax.random.fold_in(key_list[10], part), 11)
    return {
        "doc_ids": jnp.searchsorted(jnp.cumsum(ragged(part_splits[0], DOCS, TOKENS, TOKENS // 2, 2)), jnp.arange(TOKENS), side="right").astype(jnp.int32),
        "light_q": bell_draw(part_splits[1], (TOKENS, H * HD), 0.1, 0.59765625, ((0, 16), (1, 8))),
        "light_k": bell_draw(part_splits[2], (TOKENS, H * HD), 0.1, 0.59765625, ((0, 16), (1, 8))),
        "light_v": bell_draw(part_splits[3], (TOKENS, H * HD), 1.0, 6.0, ((0, 16), (1, 8))),
        "light_decay": draw_light_decay(jax.random.fold_in(key_list[10], 71), part),
        "light_grad_out": bell_draw(part_splits[5], (TOKENS, H * HD), 1.0, 6.0, ((0, 16), (1, 8))),
        "soft_q": draw_soft_q(jax.random.fold_in(jax.random.fold_in(key_list[10], part), 71), part),
        "soft_k": draw_soft_k(jax.random.fold_in(jax.random.fold_in(key_list[10], part), 71), part),
        "soft_v": bell_draw(part_splits[8], (TOKENS, H * HD), 1.0, 6.0, ((0, 16), (1, 8))),
        "soft_grad_out": bell_draw(part_splits[9], (TOKENS, H * HD), 1.0, 6.0, ((0, 16), (1, 8))),
    }


HIGHEST = lax.Precision.HIGHEST


def split_heads(whole):
    return jnp.transpose(whole.reshape(TOKENS, H, HD), (1, 0, 2))


def join_heads(parted):
    return jnp.transpose(parted, (1, 0, 2)).reshape(TOKENS, H * HD)


def reference(doc_ids, light_q, light_k, light_v, light_decay, light_grad_out, soft_q, soft_k, soft_v, soft_grad_out):
    order = jnp.arange(TOKENS, dtype=jnp.int32)
    allowed = (order[None, :] <= order[:, None]) & (doc_ids[None, :] == doc_ids[:, None])
    distance = jnp.maximum(order[:, None] - order[None, :], 0).astype(jnp.float32)
    scale = HD ** -0.5

    def light_head(inputs):
        query_half_rows, key_half_rows, value_half_rows, backward_sequence_share, slope = inputs
        query = query_half_rows.astype(jnp.float32)
        keys = key_half_rows.astype(jnp.float32)
        values = value_half_rows.astype(jnp.float32)
        grads = backward_sequence_share.astype(jnp.float32)
        weight = jnp.where(allowed, jnp.exp(-slope * distance), 0.0)
        scores = jnp.dot(query_half_rows, key_half_rows.T, preferred_element_type=jnp.float32) * weight
        output = jnp.dot(scores, values, precision=HIGHEST)
        grad_scores = jnp.dot(backward_sequence_share, value_half_rows.T, preferred_element_type=jnp.float32) * weight
        dquery = jnp.dot(grad_scores, keys, precision=HIGHEST)
        dkeys = jnp.dot(grad_scores.T, query, precision=HIGHEST)
        derivative_wrt_payloads = jnp.dot(scores.T, grads, precision=HIGHEST)
        return (output.astype(jnp.bfloat16), dquery.astype(jnp.bfloat16),
                dkeys.astype(jnp.bfloat16), derivative_wrt_payloads.astype(jnp.bfloat16))

    def soft_head(inputs):
        query, keys, values, grads = inputs
        logits = jnp.dot(query, keys.T, preferred_element_type=jnp.float32) * scale
        masked = jnp.where(allowed, logits, -1e30)
        top = jnp.max(masked, axis=1)
        raw = jnp.where(allowed, jnp.exp(masked - top[:, None]), 0.0)
        total = jnp.sum(raw, axis=1)
        expo = raw.astype(jnp.bfloat16)
        output = (jnp.dot(expo, values, preferred_element_type=jnp.float32) / total[:, None]).astype(jnp.bfloat16)
        lse = top + jnp.log(total)
        prob = jnp.where(allowed, jnp.exp(jnp.where(allowed, logits - lse[:, None], -1e30)), 0.0)
        attention_weights_bfloat16 = prob.astype(jnp.bfloat16)
        delta = jnp.sum(grads.astype(jnp.float32) * output.astype(jnp.float32), axis=1)
        derivative_wrt_payloads = jnp.dot(attention_weights_bfloat16.T, grads, preferred_element_type=jnp.float32)
        dprob = jnp.dot(grads, values.T, preferred_element_type=jnp.float32)
        dlogit = (prob * (dprob - delta[:, None])).astype(jnp.bfloat16)
        dquery = jnp.dot(dlogit, keys, preferred_element_type=jnp.float32) * scale
        dkeys = jnp.dot(dlogit.T, query, preferred_element_type=jnp.float32) * scale
        return (output, dquery.astype(jnp.bfloat16), dkeys.astype(jnp.bfloat16), derivative_wrt_payloads.astype(jnp.bfloat16))

    light = lax.map(light_head, (split_heads(light_q), split_heads(light_k), split_heads(light_v),
                                 split_heads(light_grad_out), light_decay))
    soft = lax.map(soft_head, (split_heads(soft_q), split_heads(soft_k), split_heads(soft_v),
                               split_heads(soft_grad_out)))
    return (join_heads(light[0]), join_heads(light[1]), join_heads(light[2]), join_heads(light[3]),
            join_heads(soft[0]), join_heads(soft[1]), join_heads(soft[2]), join_heads(soft[3]))
```

```python
import jax
import jax.numpy as jnp
from jax import lax
from jax.sharding import PartitionSpec as P

PRECISE = lax.Precision.HIGH
REACH = 8


def mixed(form, left, right):
    return jnp.einsum(form, left, right, precision=PRECISE, preferred_element_type=jnp.float32)


def exact(form, left, right):
    return jnp.einsum(form, left, right, preferred_element_type=jnp.float32)


def relay(value, steps, shift):
    count = lax.axis_size("seq")
    pairs = [(s, s + shift) for s in range(count) if 0 <= s + shift < count]
    out = []
    cur = value
    for _ in range(steps):
        cur = lax.ppermute(cur, "seq", pairs)
        out.append(cur)
    return out


def shifted(value, shift):
    count = lax.axis_size("seq")
    pairs = [(s, s + shift) for s in range(count) if 0 <= s + shift < count]
    return lax.ppermute(value, "seq", pairs)


def per_device(
    doc_ids,
    light_q,
    light_k,
    light_v,
    light_decay,
    light_grad_out,
    soft_q,
    soft_k,
    soft_v,
    soft_grad_out,
):
    rows = light_q.shape[0]
    heads = light_decay.shape[0]
    width = light_q.shape[1] // heads
    count = lax.axis_size("seq")
    me = lax.axis_index("seq")
    total_rows = rows * count
    reach = min(REACH, count - 1)
    span = (reach + 1) * rows
    scale = width ** (-0.5)

    all_ids = lax.all_gather(doc_ids, "seq", axis=0, tiled=True)
    local = jnp.arange(rows, dtype=jnp.int32)
    positions = me * rows + local
    head_id = doc_ids[0]
    tail_id = doc_ids[-1]
    slope = light_decay

    def shape3(a):
        return a.reshape(rows, heads, width)

    lq, lk, lv, ldo = shape3(light_q), shape3(light_k), shape3(light_v), shape3(light_grad_out)
    sq, sk, sv, sdo = shape3(soft_q), shape3(soft_k), shape3(soft_v), shape3(soft_grad_out)
    lqf, lkf, lvf, ldof = (a.astype(jnp.float32) for a in (lq, lk, lv, ldo))

    since_start = (local + 1).astype(jnp.float32)
    until_end = (rows - 1 - local).astype(jnp.float32)
    start_decay = jnp.exp(-since_start[:, None] * slope[None, :])
    end_decay = jnp.exp(-until_end[:, None] * slope[None, :])
    tail_part = end_decay * (doc_ids == tail_id)[:, None]
    head_part = start_decay * (doc_ids == head_id)[:, None]
    send_state = mixed("shk,shv->hkv", lkf * tail_part[:, :, None], lvf)
    back_state = mixed("thq,tho->hqo", lqf * head_part[:, :, None], ldof)

    fwd = relay((jnp.concatenate([soft_k, soft_v], axis=1), send_state), reach, 1)
    bwd = relay((jnp.concatenate([soft_q, soft_grad_out], axis=1), back_state), reach, -1)

    inside = (doc_ids[:, None] == doc_ids[None, :]) & (local[None, :] <= local[:, None])
    distance = jnp.maximum(local[:, None] - local[None, :], 0).astype(jnp.float32)
    weight = jnp.where(inside[None], jnp.exp(-slope[:, None, None] * distance[None]), 0.0)
    scores = exact("thd,shd->hts", lq, lk) * weight
    grad_scores = exact("thv,shv->hts", ldo, lv) * weight
    light_out = mixed("hts,shd->thd", scores, lvf)
    light_dq = mixed("hts,shk->thk", grad_scores, lkf)
    light_dk = mixed("hts,thk->shk", grad_scores, lqf)
    light_dv = mixed("hts,thv->shv", scores, ldof)

    keep = jnp.exp(-slope * rows)
    inherited = jnp.zeros_like(send_state)
    for k in range(1, reach + 1):
        source = me - k
        source_tail = all_ids[jnp.clip(source * rows + rows - 1, 0, total_rows - 1)]
        use = (source >= 0) & (source_tail == head_id)
        factor = jnp.where(use, keep ** (k - 1), 0.0)
        inherited = inherited + factor[:, None, None] * fwd[k - 1][1]
    ahead = jnp.zeros_like(back_state)
    for k in range(1, reach + 1):
        source = me + k
        source_head = all_ids[jnp.clip(source * rows, 0, total_rows - 1)]
        use = (source < count) & (source_head == tail_id)
        factor = jnp.where(use, keep ** (k - 1), 0.0)
        ahead = ahead + factor[:, None, None] * bwd[k - 1][1]
    light_out = light_out + mixed("thk,hkv->thv", lqf * head_part[:, :, None], inherited)
    light_dq = light_dq + mixed("thv,hkv->thk", ldof * head_part[:, :, None], inherited)
    light_dk = light_dk + mixed("hqo,sho->shq", ahead, lvf) * tail_part[:, :, None]
    light_dv = light_dv + mixed("hqo,shq->sho", ahead, lkf) * tail_part[:, :, None]

    key_blocks = [jnp.concatenate([soft_k, soft_v], axis=1)] + [f[0] for f in fwd]
    key_all = jnp.concatenate(key_blocks[::-1], axis=0)
    keys = key_all[:, : heads * width].reshape(span, heads, width)
    values = key_all[:, heads * width :].reshape(span, heads, width)
    key_pos = (me - reach) * rows + jnp.arange(span, dtype=jnp.int32)
    key_ids = all_ids[jnp.clip(key_pos, 0, total_rows - 1)]
    allowed = (
        (key_pos[None, :] >= 0)
        & (key_pos[None, :] <= positions[:, None])
        & (key_ids[None, :] == doc_ids[:, None])
    )[None]
    logits = exact("thd,shd->hts", sq, keys) * scale
    masked = jnp.where(allowed, logits, -1e30)
    top = jnp.max(masked, axis=2)
    raw = jnp.where(allowed, jnp.exp(masked - top[:, :, None]), 0.0)
    total = jnp.sum(raw, axis=2)
    accum = exact("hts,shd->htd", raw.astype(jnp.bfloat16), values)
    soft_out = jnp.transpose(accum / total[:, :, None], (1, 0, 2)).astype(jnp.bfloat16)
    lse = top + jnp.log(total)
    delta = jnp.sum(sdo.astype(jnp.float32) * soft_out.astype(jnp.float32), axis=2).T
    prob = jnp.where(allowed, jnp.exp(jnp.where(allowed, logits - lse[:, :, None], -1e30)), 0.0)
    dprob = exact("thd,shd->hts", sdo, values)
    dlogit = (prob * (dprob - delta[:, :, None])).astype(jnp.bfloat16)
    soft_dq = exact("hts,shd->thd", dlogit, keys) * scale

    stats = jnp.stack([lse, delta])
    stat_blocks = [stats] + [shifted(stats, -k) for k in range(1, reach + 1)]
    query_blocks = [jnp.concatenate([soft_q, soft_grad_out], axis=1)] + [b[0] for b in bwd]
    query_all = jnp.concatenate(query_blocks, axis=0)
    queries = query_all[:, : heads * width].reshape(span, heads, width)
    grads = query_all[:, heads * width :].reshape(span, heads, width)
    stat_all = jnp.concatenate(stat_blocks, axis=2)
    lse_all, delta_all = stat_all[0], stat_all[1]
    query_pos = me * rows + jnp.arange(span, dtype=jnp.int32)
    query_ids = all_ids[jnp.clip(query_pos, 0, total_rows - 1)]
    seen = (
        (query_pos[:, None] < total_rows)
        & (positions[None, :] <= query_pos[:, None])
        & (doc_ids[None, :] == query_ids[:, None])
    )[None]
    logits_t = exact("thd,shd->hts", queries, sk) * scale
    prob_t = jnp.where(seen, jnp.exp(jnp.where(seen, logits_t - lse_all[:, :, None], -1e30)), 0.0)
    soft_dv = exact("hts,thd->shd", prob_t.astype(jnp.bfloat16), grads)
    dprob_t = exact("thd,shd->hts", grads, sv)
    dlogit_t = (prob_t * (dprob_t - delta_all[:, :, None])).astype(jnp.bfloat16)
    soft_dk = exact("hts,thd->shd", dlogit_t, queries) * scale

    flat = (rows, heads * width)
    return (
        light_out.reshape(flat).astype(jnp.bfloat16),
        light_dq.reshape(flat).astype(jnp.bfloat16),
        light_dk.reshape(flat).astype(jnp.bfloat16),
        light_dv.reshape(flat).astype(jnp.bfloat16),
        soft_out.reshape(flat),
        soft_dq.reshape(flat).astype(jnp.bfloat16),
        soft_dk.reshape(flat).astype(jnp.bfloat16),
        soft_dv.reshape(flat).astype(jnp.bfloat16),
    )


def solution(mesh):
    row = P(("dp", "seq"), "head")
    return jax.shard_map(
        per_device,
        mesh=mesh,
        in_specs=(P(("dp", "seq")), row, row, row, P("head"), row, row, row, row, row),
        out_specs=(row,) * 8,
        check_vma=False,
    )
```

```python
import jax
import jax.numpy as jnp
from jax import lax
from jax.sharding import PartitionSpec as P

PRECISE = lax.Precision.HIGH
REACH = 8


def mixed(form, left, right):
    return jnp.einsum(form, left, right, precision=PRECISE, preferred_element_type=jnp.float32)


def exact(form, left, right):
    return jnp.einsum(form, left, right, preferred_element_type=jnp.float32)


def relay(value, steps, shift):
    count = lax.axis_size("seq")
    pairs = [(s, s + shift) for s in range(count) if 0 <= s + shift < count]
    out = []
    cur = value
    for _ in range(steps):
        cur = lax.ppermute(cur, "seq", pairs)
        out.append(cur)
    return out


def shifted(value, shift):
    count = lax.axis_size("seq")
    pairs = [(s, s + shift) for s in range(count) if 0 <= s + shift < count]
    return lax.ppermute(value, "seq", pairs)


def per_device(
    doc_ids,
    light_q,
    light_k,
    light_v,
    light_decay,
    light_grad_out,
    soft_q,
    soft_k,
    soft_v,
    soft_grad_out,
):
    rows = light_q.shape[0]
    heads = light_decay.shape[0]
    width = light_q.shape[1] // heads
    count = lax.axis_size("seq")
    me = lax.axis_index("seq")
    total_rows = rows * count
    reach = min(REACH, count - 1)
    span = (reach + 1) * rows
    scale = width ** (-0.5)

    local = jnp.arange(rows, dtype=jnp.int32)
    positions = me * rows + local
    head_id = doc_ids[0]
    tail_id = doc_ids[-1]
    slope = light_decay

    def shape3(a):
        return a.reshape(rows, heads, width)

    lq, lk, lv, ldo = shape3(light_q), shape3(light_k), shape3(light_v), shape3(light_grad_out)
    sq, sk, sv, sdo = shape3(soft_q), shape3(soft_k), shape3(soft_v), shape3(soft_grad_out)
    lqf, lkf, lvf, ldof = (a.astype(jnp.float32) for a in (lq, lk, lv, ldo))
    cols = heads * width
    id_cols = jnp.broadcast_to(doc_ids.astype(jnp.bfloat16)[:, None], (rows, 128))

    own_kv = jnp.concatenate([soft_k, soft_v, id_cols], axis=1)
    own_qg = jnp.concatenate([soft_q, soft_grad_out, id_cols], axis=1)
    fwd = relay(own_kv, reach, 1)
    bwd = relay(own_qg, reach, -1)

    since_start = (local + 1).astype(jnp.float32)
    until_end = (rows - 1 - local).astype(jnp.float32)
    start_decay = jnp.exp(-since_start[:, None] * slope[None, :])
    end_decay = jnp.exp(-until_end[:, None] * slope[None, :])
    tail_part = end_decay * (doc_ids == tail_id)[:, None]
    head_part = start_decay * (doc_ids == head_id)[:, None]
    send_state = mixed("shk,shv->hkv", lkf * tail_part[:, :, None], lvf)
    back_state = mixed("thq,tho->hqo", lqf * head_part[:, :, None], ldof)
    keep = jnp.exp(-slope * rows)
    head_f = head_id.astype(jnp.float32)
    tail_f = tail_id.astype(jnp.float32)

    def tagged(state, tag_a, tag_b):
        tags = jnp.zeros((heads, 8, width), jnp.float32).at[:, 0, 0].set(tag_a).at[:, 0, 1].set(tag_b)
        return jnp.concatenate([state, tags], axis=1)

    def untag(message):
        return message[:, :width], message[0, width, 0], message[0, width, 1]

    got, src_head, src_tail = untag(shifted(tagged(send_state, head_f, tail_f), 1))
    window = jnp.where((me >= 1) & (src_tail == head_f), 1.0, 0.0) * got
    step = 1
    while step < reach:
        got, src_head, _ = untag(shifted(tagged(window, head_f, tail_f), step))
        use = (me >= step) & (src_head == head_f)
        window = window + jnp.where(use, keep ** step, 0.0)[:, None, None] * got
        step *= 2
    inherited = window
    got, src_head, src_tail = untag(shifted(tagged(back_state, head_f, tail_f), -1))
    window = jnp.where((me + 1 < count) & (src_head == tail_f), 1.0, 0.0) * got
    step = 1
    while step < reach:
        got, _, src_tail = untag(shifted(tagged(window, head_f, tail_f), -step))
        use = (me + step < count) & (src_tail == tail_f)
        window = window + jnp.where(use, keep ** step, 0.0)[:, None, None] * got
        step *= 2
    ahead = window

    inside = (doc_ids[:, None] == doc_ids[None, :]) & (local[None, :] <= local[:, None])
    distance = jnp.maximum(local[:, None] - local[None, :], 0).astype(jnp.float32)
    weight = jnp.where(inside[None], jnp.exp(-slope[:, None, None] * distance[None]), 0.0)
    scores = exact("thd,shd->hts", lq, lk) * weight
    grad_scores = exact("thv,shv->hts", ldo, lv) * weight
    light_out = mixed("hts,shd->thd", scores, lvf)
    light_dq = mixed("hts,shk->thk", grad_scores, lkf)
    light_dk = mixed("hts,thk->shk", grad_scores, lqf)
    light_dv = mixed("hts,thv->shv", scores, ldof)
    light_out = light_out + mixed("thk,hkv->thv", lqf * head_part[:, :, None], inherited)
    light_dq = light_dq + mixed("thv,hkv->thk", ldof * head_part[:, :, None], inherited)
    light_dk = light_dk + mixed("hqo,sho->shq", ahead, lvf) * tail_part[:, :, None]
    light_dv = light_dv + mixed("hqo,shq->sho", ahead, lkf) * tail_part[:, :, None]

    key_all = jnp.concatenate(([own_kv] + fwd)[::-1], axis=0)
    keys = key_all[:, :cols].reshape(span, heads, width)
    values = key_all[:, cols : 2 * cols].reshape(span, heads, width)
    key_ids = key_all[:, 2 * cols].astype(jnp.int32)
    key_pos = (me - reach) * rows + jnp.arange(span, dtype=jnp.int32)
    allowed = (
        (key_pos[None, :] >= 0)
        & (key_pos[None, :] <= positions[:, None])
        & (key_ids[None, :] == doc_ids[:, None])
    )[None]
    logits = exact("thd,shd->hts", sq, keys) * scale
    masked = jnp.where(allowed, logits, -1e30)
    top = jnp.max(masked, axis=2)
    raw = jnp.where(allowed, jnp.exp(masked - top[:, :, None]), 0.0)
    total = jnp.sum(raw, axis=2)
    accum = exact("hts,shd->htd", raw.astype(jnp.bfloat16), values)
    soft_out = jnp.transpose(accum / total[:, :, None], (1, 0, 2)).astype(jnp.bfloat16)
    lse = top + jnp.log(total)
    delta = jnp.sum(sdo.astype(jnp.float32) * soft_out.astype(jnp.float32), axis=2).T
    prob = jnp.where(allowed, jnp.exp(jnp.where(allowed, logits - lse[:, :, None], -1e30)), 0.0)
    dprob = exact("thd,shd->hts", sdo, values)
    dlogit = (prob * (dprob - delta[:, :, None])).astype(jnp.bfloat16)
    soft_dq = exact("hts,shd->thd", dlogit, keys) * scale

    stats = jnp.stack([lse, delta])
    stat_blocks = [stats] + [shifted(stats, -k) for k in range(1, reach + 1)]
    query_all = jnp.concatenate([own_qg] + bwd, axis=0)
    queries = query_all[:, :cols].reshape(span, heads, width)
    grads = query_all[:, cols : 2 * cols].reshape(span, heads, width)
    query_ids = query_all[:, 2 * cols].astype(jnp.int32)
    stat_all = jnp.concatenate(stat_blocks, axis=2)
    lse_all, delta_all = stat_all[0], stat_all[1]
    query_pos = me * rows + jnp.arange(span, dtype=jnp.int32)
    seen = (
        (query_pos[:, None] < total_rows)
        & (positions[None, :] <= query_pos[:, None])
        & (doc_ids[None, :] == query_ids[:, None])
    )[None]
    logits_t = exact("thd,shd->hts", queries, sk) * scale
    prob_t = jnp.where(seen, jnp.exp(jnp.where(seen, logits_t - lse_all[:, :, None], -1e30)), 0.0)
    soft_dv = exact("hts,thd->shd", prob_t.astype(jnp.bfloat16), grads)
    dprob_t = exact("thd,shd->hts", grads, sv)
    dlogit_t = (prob_t * (dprob_t - delta_all[:, :, None])).astype(jnp.bfloat16)
    soft_dk = exact("hts,thd->shd", dlogit_t, queries) * scale

    flat = (rows, heads * width)
    return (
        light_out.reshape(flat).astype(jnp.bfloat16),
        light_dq.reshape(flat).astype(jnp.bfloat16),
        light_dk.reshape(flat).astype(jnp.bfloat16),
        light_dv.reshape(flat).astype(jnp.bfloat16),
        soft_out.reshape(flat),
        soft_dq.reshape(flat).astype(jnp.bfloat16),
        soft_dk.reshape(flat).astype(jnp.bfloat16),
        soft_dv.reshape(flat).astype(jnp.bfloat16),
    )


def solution(mesh):
    row = P(("dp", "seq"), "head")
    return jax.shard_map(
        per_device,
        mesh=mesh,
        in_specs=(P(("dp", "seq")), row, row, row, P("head"), row, row, row, row, row),
        out_specs=(row,) * 8,
        check_vma=False,
    )
```

```python
import jax
import jax.numpy as jnp
from jax import lax
from jax.sharding import PartitionSpec as P

PRECISE = lax.Precision.HIGH
REACH = 8


def mixed(form, left, right):
    return jnp.einsum(form, left, right, precision=PRECISE, preferred_element_type=jnp.float32)


def exact(form, left, right):
    return jnp.einsum(form, left, right, preferred_element_type=jnp.float32)


def relay(value, steps, shift):
    count = lax.axis_size("seq")
    pairs = [(s, s + shift) for s in range(count) if 0 <= s + shift < count]
    out = []
    cur = value
    for _ in range(steps):
        cur = lax.ppermute(cur, "seq", pairs)
        out.append(cur)
    return out


def shifted(value, shift):
    count = lax.axis_size("seq")
    pairs = [(s, s + shift) for s in range(count) if 0 <= s + shift < count]
    return lax.ppermute(value, "seq", pairs)


def swapped(value):
    count = lax.axis_size("seq")
    return lax.ppermute(value, "seq", [(s, s ^ 1) for s in range(count)])


def crossed(value, shift):
    count = lax.axis_size("seq")
    pairs = [(s, (s + shift) ^ 1) for s in range(count) if 0 <= s + shift < count]
    return lax.ppermute(value, "seq", pairs)


def per_device(
    doc_ids,
    light_q,
    light_k,
    light_v,
    light_decay,
    light_grad_out,
    soft_q,
    soft_k,
    soft_v,
    soft_grad_out,
):
    rows = light_q.shape[0]
    heads = light_decay.shape[0]
    width = light_q.shape[1] // heads
    count = lax.axis_size("seq")
    me = lax.axis_index("seq")
    total_rows = rows * count
    reach = min(REACH, count - 1)
    scale = width ** (-0.5)

    local = jnp.arange(rows, dtype=jnp.int32)
    positions = me * rows + local
    head_id = doc_ids[0]
    tail_id = doc_ids[-1]
    slope = light_decay

    def shape3(a):
        return a.reshape(rows, heads, width)

    lq, lk, lv, ldo = shape3(light_q), shape3(light_k), shape3(light_v), shape3(light_grad_out)
    sq, sk, sv, sdo = shape3(soft_q), shape3(soft_k), shape3(soft_v), shape3(soft_grad_out)
    lqf, lkf, lvf, ldof = (a.astype(jnp.float32) for a in (lq, lk, lv, ldo))
    cols = heads * width
    id_cols = jnp.broadcast_to(doc_ids.astype(jnp.bfloat16)[:, None], (rows, 128))

    own_kv = jnp.concatenate([soft_k, soft_v, id_cols], axis=1)
    own_qg = jnp.concatenate([soft_q, soft_grad_out, id_cols], axis=1)
    partner = me ^ 1

    since_start = (local + 1).astype(jnp.float32)
    until_end = (rows - 1 - local).astype(jnp.float32)
    start_decay = jnp.exp(-since_start[:, None] * slope[None, :])
    end_decay = jnp.exp(-until_end[:, None] * slope[None, :])
    tail_part = end_decay * (doc_ids == tail_id)[:, None]
    head_part = start_decay * (doc_ids == head_id)[:, None]
    send_state = mixed("shk,shv->hkv", lkf * tail_part[:, :, None], lvf)
    back_state = mixed("thq,tho->hqo", lqf * head_part[:, :, None], ldof)
    keep = jnp.exp(-slope * rows)
    head_f = head_id.astype(jnp.float32)
    tail_f = tail_id.astype(jnp.float32)

    def tagged(state, tag_a, tag_b):
        tags = jnp.zeros((heads, 8, width), jnp.float32).at[:, 0, 0].set(tag_a).at[:, 0, 1].set(tag_b)
        return jnp.concatenate([state, tags], axis=1)

    def untag(message):
        return message[:, :width], message[0, width, 0], message[0, width, 1]

    chip_hops = (reach + 1) // 2
    key_blocks = [(own_kv, me)]
    query_blocks = [(own_qg, me)]
    z_kv, z_qg = own_kv, own_qg
    fwin = bwin = None
    light_steps = [1]
    while light_steps[-1] * 2 < reach:
        light_steps.append(light_steps[-1] * 2)
    for rnd in range(chip_hops + 1):
        sent = {}
        if rnd < chip_hops:
            sent["z_kv"] = shifted(z_kv, 2)
            sent["z_qg"] = shifted(z_qg, -2)
        sent["w_kv"] = swapped(z_kv)
        sent["w_qg"] = swapped(z_qg)
        if rnd == 0:
            sent["f"] = shifted(tagged(send_state, head_f, tail_f), 1)
            sent["b"] = shifted(tagged(back_state, head_f, tail_f), -1)
        elif rnd <= len(light_steps):
            step = light_steps[rnd - 1]
            sent["f"] = shifted(tagged(fwin, head_f, tail_f), step)
            sent["b"] = shifted(tagged(bwin, head_f, tail_f), -step)
        sent = lax.optimization_barrier(sent)
        key_blocks.append((sent["w_kv"], partner - 2 * rnd))
        query_blocks.append((sent["w_qg"], partner + 2 * rnd))
        if rnd < chip_hops:
            z_kv, z_qg = sent["z_kv"], sent["z_qg"]
            key_blocks.append((z_kv, me - 2 * (rnd + 1)))
            query_blocks.append((z_qg, me + 2 * (rnd + 1)))
        if rnd == 0:
            got, _, src_tail = untag(sent["f"])
            fwin = jnp.where((me >= 1) & (src_tail == head_f), 1.0, 0.0) * got
            got, src_head, _ = untag(sent["b"])
            bwin = jnp.where((me + 1 < count) & (src_head == tail_f), 1.0, 0.0) * got
        elif rnd <= len(light_steps):
            step = light_steps[rnd - 1]
            got, src_head, _ = untag(sent["f"])
            use = (me >= step) & (src_head == head_f)
            fwin = fwin + jnp.where(use, keep ** step, 0.0)[:, None, None] * got
            got, _, src_tail = untag(sent["b"])
            use = (me + step < count) & (src_tail == tail_f)
            bwin = bwin + jnp.where(use, keep ** step, 0.0)[:, None, None] * got
    inherited = fwin
    ahead = bwin

    inside = (doc_ids[:, None] == doc_ids[None, :]) & (local[None, :] <= local[:, None])
    distance = jnp.maximum(local[:, None] - local[None, :], 0).astype(jnp.float32)
    weight = jnp.where(inside[None], jnp.exp(-slope[:, None, None] * distance[None]), 0.0)
    scores = exact("thd,shd->hts", lq, lk) * weight
    grad_scores = exact("thv,shv->hts", ldo, lv) * weight
    light_out = mixed("hts,shd->thd", scores, lvf)
    light_dq = mixed("hts,shk->thk", grad_scores, lkf)
    light_dk = mixed("hts,thk->shk", grad_scores, lqf)
    light_dv = mixed("hts,thv->shv", scores, ldof)
    light_out = light_out + mixed("thk,hkv->thv", lqf * head_part[:, :, None], inherited)
    light_dq = light_dq + mixed("thv,hkv->thk", ldof * head_part[:, :, None], inherited)
    light_dk = light_dk + mixed("hqo,sho->shq", ahead, lvf) * tail_part[:, :, None]
    light_dv = light_dv + mixed("hqo,shq->sho", ahead, lkf) * tail_part[:, :, None]

    span = len(key_blocks) * rows
    key_all = jnp.concatenate([b for b, _ in key_blocks], axis=0)
    keys = key_all[:, :cols].reshape(span, heads, width)
    values = key_all[:, cols : 2 * cols].reshape(span, heads, width)
    key_ids = key_all[:, 2 * cols].astype(jnp.int32)
    key_pos = jnp.concatenate([base * rows + local for _, base in key_blocks])
    allowed = (
        (key_pos[None, :] >= 0)
        & (key_pos[None, :] <= positions[:, None])
        & (key_ids[None, :] == doc_ids[:, None])
    )[None]
    logits = exact("thd,shd->hts", sq, keys) * scale
    masked = jnp.where(allowed, logits, -1e30)
    top = jnp.max(masked, axis=2)
    raw = jnp.where(allowed, jnp.exp(masked - top[:, :, None]), 0.0)
    total = jnp.sum(raw, axis=2)
    accum = exact("hts,shd->htd", raw.astype(jnp.bfloat16), values)
    soft_out = jnp.transpose(accum / total[:, :, None], (1, 0, 2)).astype(jnp.bfloat16)
    lse = top + jnp.log(total)
    delta = jnp.sum(sdo.astype(jnp.float32) * soft_out.astype(jnp.float32), axis=2).T
    prob = jnp.where(allowed, jnp.exp(jnp.where(allowed, logits - lse[:, :, None], -1e30)), 0.0)
    dprob = exact("thd,shd->hts", sdo, values)
    dlogit = (prob * (dprob - delta[:, :, None])).astype(jnp.bfloat16)
    soft_dq = exact("hts,shd->thd", dlogit, keys) * scale

    stats = jnp.stack([lse, delta])
    stat_blocks = [stats, swapped(stats)]
    for rnd in range(1, chip_hops + 1):
        stat_blocks.append(shifted(stats, -2 * rnd))
        stat_blocks.append(crossed(stats, -2 * rnd))
    query_all = jnp.concatenate([b for b, _ in query_blocks], axis=0)
    queries = query_all[:, :cols].reshape(span, heads, width)
    grads = query_all[:, cols : 2 * cols].reshape(span, heads, width)
    query_ids = query_all[:, 2 * cols].astype(jnp.int32)
    stat_all = jnp.concatenate(stat_blocks, axis=2)
    lse_all, delta_all = stat_all[0], stat_all[1]
    query_pos = jnp.concatenate([base * rows + local for _, base in query_blocks])
    seen = (
        (query_pos[:, None] < total_rows)
        & (positions[None, :] <= query_pos[:, None])
        & (doc_ids[None, :] == query_ids[:, None])
    )[None]
    logits_t = exact("thd,shd->hts", queries, sk) * scale
    prob_t = jnp.where(seen, jnp.exp(jnp.where(seen, logits_t - lse_all[:, :, None], -1e30)), 0.0)
    soft_dv = exact("hts,thd->shd", prob_t.astype(jnp.bfloat16), grads)
    dprob_t = exact("thd,shd->hts", grads, sv)
    dlogit_t = (prob_t * (dprob_t - delta_all[:, :, None])).astype(jnp.bfloat16)
    soft_dk = exact("hts,thd->shd", dlogit_t, queries) * scale

    flat = (rows, heads * width)
    return (
        light_out.reshape(flat).astype(jnp.bfloat16),
        light_dq.reshape(flat).astype(jnp.bfloat16),
        light_dk.reshape(flat).astype(jnp.bfloat16),
        light_dv.reshape(flat).astype(jnp.bfloat16),
        soft_out.reshape(flat),
        soft_dq.reshape(flat).astype(jnp.bfloat16),
        soft_dk.reshape(flat).astype(jnp.bfloat16),
        soft_dv.reshape(flat).astype(jnp.bfloat16),
    )


def solution(mesh):
    row = P(("dp", "seq"), "head")
    return jax.shard_map(
        per_device,
        mesh=mesh,
        in_specs=(P(("dp", "seq")), row, row, row, P("head"), row, row, row, row, row),
        out_specs=(row,) * 8,
        check_vma=False,
    )
```

```python
import jax
import jax.numpy as jnp
from jax import lax
from jax.sharding import PartitionSpec as P

PRECISE = lax.Precision.HIGH
REACH = 8


def mixed(form, left, right):
    return jnp.einsum(form, left, right, precision=PRECISE, preferred_element_type=jnp.float32)


def exact(form, left, right):
    return jnp.einsum(form, left, right, preferred_element_type=jnp.float32)


def relay(value, steps, shift):
    count = lax.axis_size("seq")
    pairs = [(s, s + shift) for s in range(count) if 0 <= s + shift < count]
    out = []
    cur = value
    for _ in range(steps):
        cur = lax.ppermute(cur, "seq", pairs)
        out.append(cur)
    return out


def shifted(value, shift):
    count = lax.axis_size("seq")
    pairs = [(s, s + shift) for s in range(count) if 0 <= s + shift < count]
    return lax.ppermute(value, "seq", pairs)


def swapped(value):
    count = lax.axis_size("seq")
    return lax.ppermute(value, "seq", [(s, s ^ 1) for s in range(count)])


def crossed(value, shift):
    count = lax.axis_size("seq")
    pairs = [(s, (s + shift) ^ 1) for s in range(count) if 0 <= s + shift < count]
    return lax.ppermute(value, "seq", pairs)


def per_device(
    doc_ids,
    light_q,
    light_k,
    light_v,
    light_decay,
    light_grad_out,
    soft_q,
    soft_k,
    soft_v,
    soft_grad_out,
):
    rows = light_q.shape[0]
    heads = light_decay.shape[0]
    width = light_q.shape[1] // heads
    count = lax.axis_size("seq")
    me = lax.axis_index("seq")
    total_rows = rows * count
    reach = min(REACH, count - 1)
    scale = width ** (-0.5)

    local = jnp.arange(rows, dtype=jnp.int32)
    positions = me * rows + local
    head_id = doc_ids[0]
    tail_id = doc_ids[-1]
    slope = light_decay

    def shape3(a):
        return a.reshape(rows, heads, width)

    lq, lk, lv, ldo = shape3(light_q), shape3(light_k), shape3(light_v), shape3(light_grad_out)
    sq, sk, sv, sdo = shape3(soft_q), shape3(soft_k), shape3(soft_v), shape3(soft_grad_out)
    lqf, lkf, lvf, ldof = (a.astype(jnp.float32) for a in (lq, lk, lv, ldo))
    cols = heads * width
    own_ids = doc_ids[None, :]

    own_kv = (jnp.concatenate([soft_k, soft_v], axis=1), own_ids)
    own_qg = (jnp.concatenate([soft_q, soft_grad_out], axis=1), own_ids)
    partner = me ^ 1

    since_start = (local + 1).astype(jnp.float32)
    until_end = (rows - 1 - local).astype(jnp.float32)
    start_decay = jnp.exp(-since_start[:, None] * slope[None, :])
    end_decay = jnp.exp(-until_end[:, None] * slope[None, :])
    tail_part = end_decay * (doc_ids == tail_id)[:, None]
    head_part = start_decay * (doc_ids == head_id)[:, None]
    send_state = mixed("shk,shv->hkv", lkf * tail_part[:, :, None], lvf)
    back_state = mixed("thq,tho->hqo", lqf * head_part[:, :, None], ldof)
    keep = jnp.exp(-slope * rows)
    head_f = head_id.astype(jnp.float32)
    tail_f = tail_id.astype(jnp.float32)

    def tagged(state, tag_a, tag_b):
        tags = jnp.zeros((heads, 8, width), jnp.float32).at[:, 0, 0].set(tag_a).at[:, 0, 1].set(tag_b)
        return jnp.concatenate([state, tags], axis=1)

    def untag(message):
        return message[:, :width], message[0, width, 0], message[0, width, 1]

    chip_hops = (reach + 1) // 2
    key_blocks = [(own_kv, me)]
    query_blocks = [(own_qg, me)]
    z_kv, z_qg = own_kv, own_qg
    fwin = bwin = None
    light_steps = [1]
    while light_steps[-1] * 2 < reach:
        light_steps.append(light_steps[-1] * 2)
    for rnd in range(chip_hops + 1):
        sent = {}
        if rnd < chip_hops:
            sent["z_kv"] = shifted(z_kv, 2)
            sent["z_qg"] = shifted(z_qg, -2)
        sent["w_kv"] = swapped(z_kv)
        sent["w_qg"] = swapped(z_qg)
        if rnd == chip_hops:
            sent["s"] = (send_state, back_state)
        sent = lax.optimization_barrier(sent)
        key_blocks.append((sent["w_kv"], partner - 2 * rnd))
        query_blocks.append((sent["w_qg"], partner + 2 * rnd))
        if rnd < chip_hops:
            z_kv, z_qg = sent["z_kv"], sent["z_qg"]
            key_blocks.append((z_kv, me - 2 * (rnd + 1)))
            query_blocks.append((z_qg, me + 2 * (rnd + 1)))
    send_state, back_state = sent["s"]
    for rnd in range(len(light_steps) + 1):
        sent = {}
        if rnd == 0:
            sent["f"] = shifted(tagged(send_state, head_f, tail_f), 1)
            sent["b"] = shifted(tagged(back_state, head_f, tail_f), -1)
        else:
            step = light_steps[rnd - 1]
            sent["f"] = shifted(tagged(fwin, head_f, tail_f), step)
            sent["b"] = shifted(tagged(bwin, head_f, tail_f), -step)
        sent = lax.optimization_barrier(sent)
        if rnd == 0:
            got, _, src_tail = untag(sent["f"])
            fwin = jnp.where((me >= 1) & (src_tail == head_f), 1.0, 0.0) * got
            got, src_head, _ = untag(sent["b"])
            bwin = jnp.where((me + 1 < count) & (src_head == tail_f), 1.0, 0.0) * got
        else:
            step = light_steps[rnd - 1]
            got, src_head, _ = untag(sent["f"])
            use = (me >= step) & (src_head == head_f)
            fwin = fwin + jnp.where(use, keep ** step, 0.0)[:, None, None] * got
            got, _, src_tail = untag(sent["b"])
            use = (me + step < count) & (src_tail == tail_f)
            bwin = bwin + jnp.where(use, keep ** step, 0.0)[:, None, None] * got
    inherited = fwin
    ahead = bwin

    inside = (doc_ids[:, None] == doc_ids[None, :]) & (local[None, :] <= local[:, None])
    distance = jnp.maximum(local[:, None] - local[None, :], 0).astype(jnp.float32)
    weight = jnp.where(inside[None], jnp.exp(-slope[:, None, None] * distance[None]), 0.0)
    scores = exact("thd,shd->hts", lq, lk) * weight
    grad_scores = exact("thv,shv->hts", ldo, lv) * weight
    light_out = mixed("hts,shd->thd", scores, lvf)
    light_dq = mixed("hts,shk->thk", grad_scores, lkf)
    light_dk = mixed("hts,thk->shk", grad_scores, lqf)
    light_dv = mixed("hts,thv->shv", scores, ldof)
    light_out = light_out + mixed("thk,hkv->thv", lqf * head_part[:, :, None], inherited)
    light_dq = light_dq + mixed("thv,hkv->thk", ldof * head_part[:, :, None], inherited)
    light_dk = light_dk + mixed("hqo,sho->shq", ahead, lvf) * tail_part[:, :, None]
    light_dv = light_dv + mixed("hqo,shq->sho", ahead, lkf) * tail_part[:, :, None]

    span = len(key_blocks) * rows
    key_all = jnp.concatenate([b for (b, _), _ in key_blocks], axis=0)
    keys = key_all[:, :cols].reshape(span, heads, width)
    values = key_all[:, cols : 2 * cols].reshape(span, heads, width)
    key_ids = jnp.concatenate([i[0] for (_, i), _ in key_blocks])
    key_pos = jnp.concatenate([base * rows + local for _, base in key_blocks])
    allowed = (
        (key_pos[None, :] >= 0)
        & (key_pos[None, :] <= positions[:, None])
        & (key_ids[None, :] == doc_ids[:, None])
    )[None]
    logits = exact("thd,shd->hts", sq, keys) * scale
    masked = jnp.where(allowed, logits, -1e30)
    top = jnp.max(masked, axis=2)
    raw = jnp.where(allowed, jnp.exp(masked - top[:, :, None]), 0.0)
    total = jnp.sum(raw, axis=2)
    accum = exact("hts,shd->htd", raw.astype(jnp.bfloat16), values)
    soft_out = jnp.transpose(accum / total[:, :, None], (1, 0, 2)).astype(jnp.bfloat16)
    lse = top + jnp.log(total)
    delta = jnp.sum(sdo.astype(jnp.float32) * soft_out.astype(jnp.float32), axis=2).T
    prob = jnp.where(allowed, jnp.exp(jnp.where(allowed, logits - lse[:, :, None], -1e30)), 0.0)
    dprob = exact("thd,shd->hts", sdo, values)
    dlogit = (prob * (dprob - delta[:, :, None])).astype(jnp.bfloat16)
    soft_dq = exact("hts,shd->thd", dlogit, keys) * scale

    stats = jnp.stack([lse, delta])
    stat_blocks = [stats, swapped(stats)]
    for rnd in range(1, chip_hops + 1):
        stat_blocks.append(shifted(stats, -2 * rnd))
        stat_blocks.append(crossed(stats, -2 * rnd))
    query_all = jnp.concatenate([b for (b, _), _ in query_blocks], axis=0)
    queries = query_all[:, :cols].reshape(span, heads, width)
    grads = query_all[:, cols : 2 * cols].reshape(span, heads, width)
    query_ids = jnp.concatenate([i[0] for (_, i), _ in query_blocks])
    stat_all = jnp.concatenate(stat_blocks, axis=2)
    lse_all, delta_all = stat_all[0], stat_all[1]
    query_pos = jnp.concatenate([base * rows + local for _, base in query_blocks])
    seen = (
        (query_pos[:, None] < total_rows)
        & (positions[None, :] <= query_pos[:, None])
        & (doc_ids[None, :] == query_ids[:, None])
    )[None]
    logits_t = exact("thd,shd->hts", queries, sk) * scale
    prob_t = jnp.where(seen, jnp.exp(jnp.where(seen, logits_t - lse_all[:, :, None], -1e30)), 0.0)
    soft_dv = exact("hts,thd->shd", prob_t.astype(jnp.bfloat16), grads)
    dprob_t = exact("thd,shd->hts", grads, sv)
    dlogit_t = (prob_t * (dprob_t - delta_all[:, :, None])).astype(jnp.bfloat16)
    soft_dk = exact("hts,thd->shd", dlogit_t, queries) * scale

    flat = (rows, heads * width)
    return (
        light_out.reshape(flat).astype(jnp.bfloat16),
        light_dq.reshape(flat).astype(jnp.bfloat16),
        light_dk.reshape(flat).astype(jnp.bfloat16),
        light_dv.reshape(flat).astype(jnp.bfloat16),
        soft_out.reshape(flat),
        soft_dq.reshape(flat).astype(jnp.bfloat16),
        soft_dk.reshape(flat).astype(jnp.bfloat16),
        soft_dv.reshape(flat).astype(jnp.bfloat16),
    )


def solution(mesh):
    row = P(("dp", "seq"), "head")
    return jax.shard_map(
        per_device,
        mesh=mesh,
        in_specs=(P(("dp", "seq")), row, row, row, P("head"), row, row, row, row, row),
        out_specs=(row,) * 8,
        check_vma=False,
    )
```

```python
import jax
import jax.numpy as jnp
from jax import lax
from jax.sharding import PartitionSpec as P

PRECISE = lax.Precision.HIGH
REACH = 8


def mixed(form, left, right):
    return jnp.einsum(form, left, right, precision=PRECISE, preferred_element_type=jnp.float32)


def exact(form, left, right):
    return jnp.einsum(form, left, right, preferred_element_type=jnp.float32)


def relay(value, steps, shift):
    count = lax.axis_size("seq")
    pairs = [(s, s + shift) for s in range(count) if 0 <= s + shift < count]
    out = []
    cur = value
    for _ in range(steps):
        cur = lax.ppermute(cur, "seq", pairs)
        out.append(cur)
    return out


def shifted(value, shift):
    count = lax.axis_size("seq")
    pairs = [(s, s + shift) for s in range(count) if 0 <= s + shift < count]
    return lax.ppermute(value, "seq", pairs)


def swapped(value):
    count = lax.axis_size("seq")
    return lax.ppermute(value, "seq", [(s, s ^ 1) for s in range(count)])


def crossed(value, shift):
    count = lax.axis_size("seq")
    pairs = [(s, (s + shift) ^ 1) for s in range(count) if 0 <= s + shift < count]
    return lax.ppermute(value, "seq", pairs)


def per_device(
    doc_ids,
    light_q,
    light_k,
    light_v,
    light_decay,
    light_grad_out,
    soft_q,
    soft_k,
    soft_v,
    soft_grad_out,
):
    rows = light_q.shape[0]
    heads = light_decay.shape[0]
    width = light_q.shape[1] // heads
    count = lax.axis_size("seq")
    me = lax.axis_index("seq")
    total_rows = rows * count
    reach = min(REACH, count - 1)
    scale = width ** (-0.5)

    local = jnp.arange(rows, dtype=jnp.int32)
    positions = me * rows + local
    head_id = doc_ids[0]
    tail_id = doc_ids[-1]
    slope = light_decay

    def shape3(a):
        return a.reshape(rows, heads, width)

    lq, lk, lv, ldo = shape3(light_q), shape3(light_k), shape3(light_v), shape3(light_grad_out)
    sq, sk, sv, sdo = shape3(soft_q), shape3(soft_k), shape3(soft_v), shape3(soft_grad_out)
    lqf, lkf, lvf, ldof = (a.astype(jnp.float32) for a in (lq, lk, lv, ldo))
    cols = heads * width
    own_ids = doc_ids[None, :]

    own_kv = (jnp.concatenate([soft_k, soft_v], axis=1), own_ids)
    own_qg = (jnp.concatenate([soft_q, soft_grad_out], axis=1), own_ids)
    partner = me ^ 1

    since_start = (local + 1).astype(jnp.float32)
    until_end = (rows - 1 - local).astype(jnp.float32)
    start_decay = jnp.exp(-since_start[:, None] * slope[None, :])
    end_decay = jnp.exp(-until_end[:, None] * slope[None, :])
    tail_part = end_decay * (doc_ids == tail_id)[:, None]
    head_part = start_decay * (doc_ids == head_id)[:, None]
    send_state = mixed("shk,shv->hkv", lkf * tail_part[:, :, None], lvf)
    back_state = mixed("thq,tho->hqo", lqf * head_part[:, :, None], ldof)
    keep = jnp.exp(-slope * rows)
    head_f = head_id.astype(jnp.float32)
    tail_f = tail_id.astype(jnp.float32)

    def tagged(state, tag_a, tag_b):
        tags = jnp.zeros((heads, 8, width), jnp.float32).at[:, 0, 0].set(tag_a).at[:, 0, 1].set(tag_b)
        return jnp.concatenate([state, tags], axis=1)

    def untag(message):
        return message[:, :width], message[0, width, 0], message[0, width, 1]

    chip_hops = (reach + 1) // 2
    key_blocks = [(own_kv, me)]
    query_blocks = [(own_qg, me)]
    z_kv, z_qg = own_kv, own_qg
    fwin = bwin = None
    light_steps = [1]
    while light_steps[-1] * 2 < reach:
        light_steps.append(light_steps[-1] * 2)
    for rnd in range(chip_hops + 1):
        sent = {}
        if rnd < chip_hops:
            sent["z_kv"] = shifted(z_kv, 2)
            sent["z_qg"] = shifted(z_qg, -2)
        sent["w_kv"] = swapped(z_kv)
        sent["w_qg"] = swapped(z_qg)
        if rnd == 0:
            sent["f"] = shifted(tagged(send_state, head_f, tail_f).astype(jnp.bfloat16), 1)
            sent["b"] = shifted(tagged(back_state, head_f, tail_f).astype(jnp.bfloat16), -1)
        elif rnd <= len(light_steps):
            step = light_steps[rnd - 1]
            sent["f"] = shifted(tagged(fwin, head_f, tail_f).astype(jnp.bfloat16), step)
            sent["b"] = shifted(tagged(bwin, head_f, tail_f).astype(jnp.bfloat16), -step)
        sent = lax.optimization_barrier(sent)
        key_blocks.append((sent["w_kv"], partner - 2 * rnd))
        query_blocks.append((sent["w_qg"], partner + 2 * rnd))
        if rnd < chip_hops:
            z_kv, z_qg = sent["z_kv"], sent["z_qg"]
            key_blocks.append((z_kv, me - 2 * (rnd + 1)))
            query_blocks.append((z_qg, me + 2 * (rnd + 1)))
        if rnd == 0:
            got, _, src_tail = untag(sent["f"].astype(jnp.float32))
            fwin = jnp.where((me >= 1) & (src_tail == head_f), 1.0, 0.0) * got
            got, src_head, _ = untag(sent["b"].astype(jnp.float32))
            bwin = jnp.where((me + 1 < count) & (src_head == tail_f), 1.0, 0.0) * got
        elif rnd <= len(light_steps):
            step = light_steps[rnd - 1]
            got, src_head, _ = untag(sent["f"].astype(jnp.float32))
            use = (me >= step) & (src_head == head_f)
            fwin = fwin + jnp.where(use, keep ** step, 0.0)[:, None, None] * got
            got, _, src_tail = untag(sent["b"].astype(jnp.float32))
            use = (me + step < count) & (src_tail == tail_f)
            bwin = bwin + jnp.where(use, keep ** step, 0.0)[:, None, None] * got
    inherited = fwin
    ahead = bwin

    inside = (doc_ids[:, None] == doc_ids[None, :]) & (local[None, :] <= local[:, None])
    distance = jnp.maximum(local[:, None] - local[None, :], 0).astype(jnp.float32)
    weight = jnp.where(inside[None], jnp.exp(-slope[:, None, None] * distance[None]), 0.0)
    scores = exact("thd,shd->hts", lq, lk) * weight
    grad_scores = exact("thv,shv->hts", ldo, lv) * weight
    light_out = mixed("hts,shd->thd", scores, lvf)
    light_dq = mixed("hts,shk->thk", grad_scores, lkf)
    light_dk = mixed("hts,thk->shk", grad_scores, lqf)
    light_dv = mixed("hts,thv->shv", scores, ldof)
    light_out = light_out + mixed("thk,hkv->thv", lqf * head_part[:, :, None], inherited)
    light_dq = light_dq + mixed("thv,hkv->thk", ldof * head_part[:, :, None], inherited)
    light_dk = light_dk + mixed("hqo,sho->shq", ahead, lvf) * tail_part[:, :, None]
    light_dv = light_dv + mixed("hqo,shq->sho", ahead, lkf) * tail_part[:, :, None]

    span = len(key_blocks) * rows
    key_all = jnp.concatenate([b for (b, _), _ in key_blocks], axis=0)
    keys = key_all[:, :cols].reshape(span, heads, width)
    values = key_all[:, cols : 2 * cols].reshape(span, heads, width)
    key_ids = jnp.concatenate([i[0] for (_, i), _ in key_blocks])
    key_pos = jnp.concatenate([base * rows + local for _, base in key_blocks])
    allowed = (
        (key_pos[None, :] >= 0)
        & (key_pos[None, :] <= positions[:, None])
        & (key_ids[None, :] == doc_ids[:, None])
    )[None]
    logits = exact("thd,shd->hts", sq, keys) * scale
    masked = jnp.where(allowed, logits, -1e30)
    top = jnp.max(masked, axis=2)
    raw = jnp.where(allowed, jnp.exp(masked - top[:, :, None]), 0.0)
    total = jnp.sum(raw, axis=2)
    accum = exact("hts,shd->htd", raw.astype(jnp.bfloat16), values)
    soft_out = jnp.transpose(accum / total[:, :, None], (1, 0, 2)).astype(jnp.bfloat16)
    lse = top + jnp.log(total)
    delta = jnp.sum(sdo.astype(jnp.float32) * soft_out.astype(jnp.float32), axis=2).T
    prob = jnp.where(allowed, jnp.exp(jnp.where(allowed, logits - lse[:, :, None], -1e30)), 0.0)
    dprob = exact("thd,shd->hts", sdo, values)
    dlogit = (prob * (dprob - delta[:, :, None])).astype(jnp.bfloat16)
    soft_dq = exact("hts,shd->thd", dlogit, keys) * scale

    stats = jnp.stack([lse, delta])
    stat_blocks = [stats, swapped(stats)]
    for rnd in range(1, chip_hops + 1):
        stat_blocks.append(shifted(stats, -2 * rnd))
        stat_blocks.append(crossed(stats, -2 * rnd))
    query_all = jnp.concatenate([b for (b, _), _ in query_blocks], axis=0)
    queries = query_all[:, :cols].reshape(span, heads, width)
    grads = query_all[:, cols : 2 * cols].reshape(span, heads, width)
    query_ids = jnp.concatenate([i[0] for (_, i), _ in query_blocks])
    stat_all = jnp.concatenate(stat_blocks, axis=2)
    lse_all, delta_all = stat_all[0], stat_all[1]
    query_pos = jnp.concatenate([base * rows + local for _, base in query_blocks])
    seen = (
        (query_pos[:, None] < total_rows)
        & (positions[None, :] <= query_pos[:, None])
        & (doc_ids[None, :] == query_ids[:, None])
    )[None]
    logits_t = exact("thd,shd->hts", queries, sk) * scale
    prob_t = jnp.where(seen, jnp.exp(jnp.where(seen, logits_t - lse_all[:, :, None], -1e30)), 0.0)
    soft_dv = exact("hts,thd->shd", prob_t.astype(jnp.bfloat16), grads)
    dprob_t = exact("thd,shd->hts", grads, sv)
    dlogit_t = (prob_t * (dprob_t - delta_all[:, :, None])).astype(jnp.bfloat16)
    soft_dk = exact("hts,thd->shd", dlogit_t, queries) * scale

    flat = (rows, heads * width)
    return (
        light_out.reshape(flat).astype(jnp.bfloat16),
        light_dq.reshape(flat).astype(jnp.bfloat16),
        light_dk.reshape(flat).astype(jnp.bfloat16),
        light_dv.reshape(flat).astype(jnp.bfloat16),
        soft_out.reshape(flat),
        soft_dq.reshape(flat).astype(jnp.bfloat16),
        soft_dk.reshape(flat).astype(jnp.bfloat16),
        soft_dv.reshape(flat).astype(jnp.bfloat16),
    )


def solution(mesh):
    row = P(("dp", "seq"), "head")
    return jax.shard_map(
        per_device,
        mesh=mesh,
        in_specs=(P(("dp", "seq")), row, row, row, P("head"), row, row, row, row, row),
        out_specs=(row,) * 8,
        check_vma=False,
    )
```

```python
import jax
import jax.numpy as jnp
from jax import lax
from jax.sharding import PartitionSpec as P

PRECISE = lax.Precision.HIGH
REACH = 8


def mixed(form, left, right):
    return jnp.einsum(form, left, right, precision=PRECISE, preferred_element_type=jnp.float32)


def exact(form, left, right):
    return jnp.einsum(form, left, right, preferred_element_type=jnp.float32)


def relay(value, steps, shift):
    count = lax.axis_size("seq")
    pairs = [(s, s + shift) for s in range(count) if 0 <= s + shift < count]
    out = []
    cur = value
    for _ in range(steps):
        cur = lax.ppermute(cur, "seq", pairs)
        out.append(cur)
    return out


def shifted(value, shift):
    count = lax.axis_size("seq")
    pairs = [(s, s + shift) for s in range(count) if 0 <= s + shift < count]
    return lax.ppermute(value, "seq", pairs)


def swapped(value):
    count = lax.axis_size("seq")
    return lax.ppermute(value, "seq", [(s, s ^ 1) for s in range(count)])


def crossed(value, shift):
    count = lax.axis_size("seq")
    pairs = [(s, (s + shift) ^ 1) for s in range(count) if 0 <= s + shift < count]
    return lax.ppermute(value, "seq", pairs)


def per_device(
    doc_ids,
    light_q,
    light_k,
    light_v,
    light_decay,
    light_grad_out,
    soft_q,
    soft_k,
    soft_v,
    soft_grad_out,
):
    rows = light_q.shape[0]
    heads = light_decay.shape[0]
    width = light_q.shape[1] // heads
    count = lax.axis_size("seq")
    me = lax.axis_index("seq")
    total_rows = rows * count
    reach = min(REACH, count - 1)
    scale = width ** (-0.5)

    local = jnp.arange(rows, dtype=jnp.int32)
    positions = me * rows + local
    head_id = doc_ids[0]
    tail_id = doc_ids[-1]
    slope = light_decay

    def shape3(a):
        return a.reshape(rows, heads, width)

    lq, lk, lv, ldo = shape3(light_q), shape3(light_k), shape3(light_v), shape3(light_grad_out)
    sq, sk, sv, sdo = shape3(soft_q), shape3(soft_k), shape3(soft_v), shape3(soft_grad_out)
    lqf, lkf, lvf, ldof = (a.astype(jnp.float32) for a in (lq, lk, lv, ldo))
    cols = heads * width
    own_ids = doc_ids[None, :]

    own_kv = (jnp.concatenate([soft_k, soft_v], axis=1), own_ids)
    own_qg = (jnp.concatenate([soft_q, soft_grad_out], axis=1), own_ids)
    partner = me ^ 1

    since_start = (local + 1).astype(jnp.float32)
    until_end = (rows - 1 - local).astype(jnp.float32)
    start_decay = jnp.exp(-since_start[:, None] * slope[None, :])
    end_decay = jnp.exp(-until_end[:, None] * slope[None, :])
    tail_part = end_decay * (doc_ids == tail_id)[:, None]
    head_part = start_decay * (doc_ids == head_id)[:, None]
    send_state = mixed("shk,shv->hkv", lkf * tail_part[:, :, None], lvf)
    back_state = mixed("thq,tho->hqo", lqf * head_part[:, :, None], ldof)
    keep = jnp.exp(-slope * rows)
    head_f = head_id.astype(jnp.float32)
    tail_f = tail_id.astype(jnp.float32)

    def tagged(state, tag_a, tag_b):
        tags = jnp.zeros((heads, 8, width), jnp.float32).at[:, 0, 0].set(tag_a).at[:, 0, 1].set(tag_b)
        return jnp.concatenate([state, tags], axis=1)

    def untag(message):
        return message[:, :width], message[0, width, 0], message[0, width, 1]

    chip_hops = (reach + 1) // 2
    key_blocks = [(own_kv, me)]
    query_blocks = [(own_qg, me)]
    z_kv, z_qg = own_kv, own_qg
    fwin = bwin = None
    light_steps = [1]
    while light_steps[-1] * 2 < reach:
        light_steps.append(light_steps[-1] * 2)
    def key_first(block, base):
        (kv, ids), = (block,)
        kb = kv[:, :cols].reshape(rows, heads, width)
        vb = kv[:, cols:].reshape(rows, heads, width)
        kpos = base * rows + local
        allowed = (
            (kpos[None, :] >= 0) & (kpos[None, :] <= positions[:, None]) & (ids[0][None, :] == doc_ids[:, None])
        )[None]
        masked = jnp.where(allowed, exact("thd,shd->hts", sq, kb) * scale, -1e30)
        return masked, jnp.max(masked, axis=2), exact("thd,shd->hts", sdo, vb)

    def query_first(block, base):
        (qg, ids), = (block,)
        qb = qg[:, :cols].reshape(rows, heads, width)
        gb = qg[:, cols:].reshape(rows, heads, width)
        qpos = base * rows + local
        seen = (
            (qpos[:, None] < total_rows)
            & (positions[None, :] <= qpos[:, None])
            & (doc_ids[None, :] == ids[0][:, None])
        )[None]
        masked = jnp.where(seen, exact("thd,shd->hts", qb, sk) * scale, -1e30)
        return masked, exact("thd,shd->hts", gb, sv)

    key_first_done = []
    query_first_done = []
    pending = {"k": [key_first(own_kv, me)], "q": [query_first(own_qg, me)]}
    for rnd in range(chip_hops + 1):
        sent = {}
        sent["pend"] = pending
        if rnd < chip_hops:
            sent["z_kv"] = shifted(z_kv, 2)
            sent["z_qg"] = shifted(z_qg, -2)
        sent["w_kv"] = swapped(z_kv)
        sent["w_qg"] = swapped(z_qg)
        if rnd == 0:
            sent["f"] = shifted(tagged(send_state, head_f, tail_f).astype(jnp.bfloat16), 1)
            sent["b"] = shifted(tagged(back_state, head_f, tail_f).astype(jnp.bfloat16), -1)
        elif rnd <= len(light_steps):
            step = light_steps[rnd - 1]
            sent["f"] = shifted(tagged(fwin, head_f, tail_f).astype(jnp.bfloat16), step)
            sent["b"] = shifted(tagged(bwin, head_f, tail_f).astype(jnp.bfloat16), -step)
        sent = lax.optimization_barrier(sent)
        key_first_done += sent["pend"]["k"]
        query_first_done += sent["pend"]["q"]
        fresh_k = [(sent["w_kv"], partner - 2 * rnd)]
        fresh_q = [(sent["w_qg"], partner + 2 * rnd)]
        if rnd < chip_hops:
            z_kv, z_qg = sent["z_kv"], sent["z_qg"]
            fresh_k.append((z_kv, me - 2 * (rnd + 1)))
            fresh_q.append((z_qg, me + 2 * (rnd + 1)))
        key_blocks += fresh_k
        query_blocks += fresh_q
        pending = {"k": [key_first(b, base) for b, base in fresh_k], "q": [query_first(b, base) for b, base in fresh_q]}
        if rnd == 0:
            got, _, src_tail = untag(sent["f"].astype(jnp.float32))
            fwin = jnp.where((me >= 1) & (src_tail == head_f), 1.0, 0.0) * got
            got, src_head, _ = untag(sent["b"].astype(jnp.float32))
            bwin = jnp.where((me + 1 < count) & (src_head == tail_f), 1.0, 0.0) * got
        elif rnd <= len(light_steps):
            step = light_steps[rnd - 1]
            got, src_head, _ = untag(sent["f"].astype(jnp.float32))
            use = (me >= step) & (src_head == head_f)
            fwin = fwin + jnp.where(use, keep ** step, 0.0)[:, None, None] * got
            got, _, src_tail = untag(sent["b"].astype(jnp.float32))
            use = (me + step < count) & (src_tail == tail_f)
            bwin = bwin + jnp.where(use, keep ** step, 0.0)[:, None, None] * got
    inherited = fwin
    ahead = bwin

    inside = (doc_ids[:, None] == doc_ids[None, :]) & (local[None, :] <= local[:, None])
    distance = jnp.maximum(local[:, None] - local[None, :], 0).astype(jnp.float32)
    weight = jnp.where(inside[None], jnp.exp(-slope[:, None, None] * distance[None]), 0.0)
    scores = exact("thd,shd->hts", lq, lk) * weight
    grad_scores = exact("thv,shv->hts", ldo, lv) * weight
    light_out = mixed("hts,shd->thd", scores, lvf)
    light_dq = mixed("hts,shk->thk", grad_scores, lkf)
    light_dk = mixed("hts,thk->shk", grad_scores, lqf)
    light_dv = mixed("hts,thv->shv", scores, ldof)
    light_out = light_out + mixed("thk,hkv->thv", lqf * head_part[:, :, None], inherited)
    light_dq = light_dq + mixed("thv,hkv->thk", ldof * head_part[:, :, None], inherited)
    light_dk = light_dk + mixed("hqo,sho->shq", ahead, lvf) * tail_part[:, :, None]
    light_dv = light_dv + mixed("hqo,shq->sho", ahead, lkf) * tail_part[:, :, None]

    key_first_done += pending["k"]
    query_first_done += pending["q"]

    top = key_first_done[0][1]
    for _, block_top, _ in key_first_done[1:]:
        top = jnp.maximum(top, block_top)
    total = jnp.zeros_like(top)
    accum = jnp.zeros((heads, rows, width), jnp.float32)
    for ((kv, _), _), (masked, _, _) in zip(key_blocks, key_first_done):
        vb = kv[:, cols:].reshape(rows, heads, width)
        raw = jnp.where(masked > -1e29, jnp.exp(masked - top[:, :, None]), 0.0)
        total = total + jnp.sum(raw, axis=2)
        accum = accum + exact("hts,shd->htd", raw.astype(jnp.bfloat16), vb)
    soft_out = jnp.transpose(accum / total[:, :, None], (1, 0, 2)).astype(jnp.bfloat16)
    lse = top + jnp.log(total)
    delta = jnp.sum(sdo.astype(jnp.float32) * soft_out.astype(jnp.float32), axis=2).T
    soft_dq = jnp.zeros((rows, heads, width), jnp.float32)
    for ((kv, _), _), (masked, _, dprob) in zip(key_blocks, key_first_done):
        kb = kv[:, :cols].reshape(rows, heads, width)
        prob = jnp.where(masked > -1e29, jnp.exp(masked - lse[:, :, None]), 0.0)
        dlogit = (prob * (dprob - delta[:, :, None])).astype(jnp.bfloat16)
        soft_dq = soft_dq + exact("hts,shd->thd", dlogit, kb)
    soft_dq = soft_dq * scale

    stats = jnp.stack([lse, delta])
    stat_blocks = [stats, swapped(stats)]
    for rnd in range(1, chip_hops + 1):
        stat_blocks.append(shifted(stats, -2 * rnd))
        stat_blocks.append(crossed(stats, -2 * rnd))
    soft_dk = jnp.zeros((rows, heads, width), jnp.float32)
    soft_dv = jnp.zeros((rows, heads, width), jnp.float32)
    for ((qg, _), _), (masked, dprob), stat in zip(query_blocks, query_first_done, stat_blocks):
        qb = qg[:, :cols].reshape(rows, heads, width)
        gb = qg[:, cols:].reshape(rows, heads, width)
        prob = jnp.where(masked > -1e29, jnp.exp(masked - stat[0][:, :, None]), 0.0)
        soft_dv = soft_dv + exact("hts,thd->shd", prob.astype(jnp.bfloat16), gb)
        dlogit = (prob * (dprob - stat[1][:, :, None])).astype(jnp.bfloat16)
        soft_dk = soft_dk + exact("hts,thd->shd", dlogit, qb)
    soft_dk = soft_dk * scale

    flat = (rows, heads * width)
    return (
        light_out.reshape(flat).astype(jnp.bfloat16),
        light_dq.reshape(flat).astype(jnp.bfloat16),
        light_dk.reshape(flat).astype(jnp.bfloat16),
        light_dv.reshape(flat).astype(jnp.bfloat16),
        soft_out.reshape(flat),
        soft_dq.reshape(flat).astype(jnp.bfloat16),
        soft_dk.reshape(flat).astype(jnp.bfloat16),
        soft_dv.reshape(flat).astype(jnp.bfloat16),
    )


def solution(mesh):
    row = P(("dp", "seq"), "head")
    return jax.shard_map(
        per_device,
        mesh=mesh,
        in_specs=(P(("dp", "seq")), row, row, row, P("head"), row, row, row, row, row),
        out_specs=(row,) * 8,
        check_vma=False,
    )
```

```python
import jax
import jax.numpy as jnp
from jax import lax
from jax.sharding import PartitionSpec as P

PRECISE = lax.Precision.HIGH
REACH = 8


def mixed(form, left, right):
    return jnp.einsum(form, left, right, precision=PRECISE, preferred_element_type=jnp.float32)


def exact(form, left, right):
    return jnp.einsum(form, left, right, preferred_element_type=jnp.float32)


def relay(value, steps, shift):
    count = lax.axis_size("seq")
    pairs = [(s, s + shift) for s in range(count) if 0 <= s + shift < count]
    out = []
    cur = value
    for _ in range(steps):
        cur = lax.ppermute(cur, "seq", pairs)
        out.append(cur)
    return out


def shifted(value, shift):
    count = lax.axis_size("seq")
    pairs = [(s, s + shift) for s in range(count) if 0 <= s + shift < count]
    return lax.ppermute(value, "seq", pairs)


def swapped(value):
    count = lax.axis_size("seq")
    return lax.ppermute(value, "seq", [(s, s ^ 1) for s in range(count)])


def crossed(value, shift):
    count = lax.axis_size("seq")
    pairs = [(s, (s + shift) ^ 1) for s in range(count) if 0 <= s + shift < count]
    return lax.ppermute(value, "seq", pairs)


def per_device(
    doc_ids,
    light_q,
    light_k,
    light_v,
    light_decay,
    light_grad_out,
    soft_q,
    soft_k,
    soft_v,
    soft_grad_out,
):
    rows = light_q.shape[0]
    heads = light_decay.shape[0]
    width = light_q.shape[1] // heads
    count = lax.axis_size("seq")
    me = lax.axis_index("seq")
    total_rows = rows * count
    reach = min(REACH, count - 1)
    scale = width ** (-0.5)

    local = jnp.arange(rows, dtype=jnp.int32)
    positions = me * rows + local
    head_id = doc_ids[0]
    tail_id = doc_ids[-1]
    slope = light_decay

    def shape3(a):
        return a.reshape(rows, heads, width)

    lq, lk, lv, ldo = shape3(light_q), shape3(light_k), shape3(light_v), shape3(light_grad_out)
    sq, sk, sv, sdo = shape3(soft_q), shape3(soft_k), shape3(soft_v), shape3(soft_grad_out)
    lqf, lkf, lvf, ldof = (a.astype(jnp.float32) for a in (lq, lk, lv, ldo))
    cols = heads * width
    own_ids = doc_ids[None, :]

    own_kv = (jnp.concatenate([soft_k, soft_v], axis=1), own_ids)
    own_qg = (jnp.concatenate([soft_q, soft_grad_out], axis=1), own_ids)
    partner = me ^ 1

    since_start = (local + 1).astype(jnp.float32)
    until_end = (rows - 1 - local).astype(jnp.float32)
    start_decay = jnp.exp(-since_start[:, None] * slope[None, :])
    end_decay = jnp.exp(-until_end[:, None] * slope[None, :])
    tail_part = end_decay * (doc_ids == tail_id)[:, None]
    head_part = start_decay * (doc_ids == head_id)[:, None]
    send_state = mixed("shk,shv->hkv", lkf * tail_part[:, :, None], lvf)
    back_state = mixed("thq,tho->hqo", lqf * head_part[:, :, None], ldof)
    keep = jnp.exp(-slope * rows)
    head_f = head_id.astype(jnp.float32)
    tail_f = tail_id.astype(jnp.float32)

    def tagged(state, tag_a, tag_b):
        tags = jnp.zeros((heads, 8, width), jnp.float32).at[:, 0, 0].set(tag_a).at[:, 0, 1].set(tag_b)
        return jnp.concatenate([state, tags], axis=1)

    def untag(message):
        return message[:, :width], message[0, width, 0], message[0, width, 1]

    chip_hops = (reach + 1) // 2
    key_blocks = [(own_kv, me)]
    query_blocks = [(own_qg, me)]
    z_kv, z_qg = own_kv, own_qg
    fwin = bwin = None
    light_steps = [1]
    while light_steps[-1] * 2 < reach:
        light_steps.append(light_steps[-1] * 2)
    for rnd in range(chip_hops + 1):
        sent = {}
        if rnd < chip_hops:
            sent["z_kv"] = shifted(z_kv, 2)
            sent["z_qg"] = shifted(z_qg, -2)
        sent["w_kv"] = swapped(z_kv)
        sent["w_qg"] = swapped(z_qg)
        if rnd == 0:
            sent["f"] = shifted(tagged(send_state, head_f, tail_f).astype(jnp.bfloat16), 1)
            sent["b"] = shifted(tagged(back_state, head_f, tail_f).astype(jnp.bfloat16), -1)
        elif rnd <= len(light_steps):
            step = light_steps[rnd - 1]
            sent["f"] = shifted(tagged(fwin, head_f, tail_f).astype(jnp.bfloat16), step)
            sent["b"] = shifted(tagged(bwin, head_f, tail_f).astype(jnp.bfloat16), -step)
        sent = lax.optimization_barrier(sent)
        key_blocks.append((sent["w_kv"], partner - 2 * rnd))
        query_blocks.append((sent["w_qg"], partner + 2 * rnd))
        if rnd < chip_hops:
            z_kv, z_qg = sent["z_kv"], sent["z_qg"]
            key_blocks.append((z_kv, me - 2 * (rnd + 1)))
            query_blocks.append((z_qg, me + 2 * (rnd + 1)))
        if rnd == 0:
            got, _, src_tail = untag(sent["f"].astype(jnp.float32))
            fwin = jnp.where((me >= 1) & (src_tail == head_f), 1.0, 0.0) * got
            got, src_head, _ = untag(sent["b"].astype(jnp.float32))
            bwin = jnp.where((me + 1 < count) & (src_head == tail_f), 1.0, 0.0) * got
        elif rnd <= len(light_steps):
            step = light_steps[rnd - 1]
            got, src_head, _ = untag(sent["f"].astype(jnp.float32))
            use = (me >= step) & (src_head == head_f)
            fwin = fwin + jnp.where(use, keep ** step, 0.0)[:, None, None] * got
            got, _, src_tail = untag(sent["b"].astype(jnp.float32))
            use = (me + step < count) & (src_tail == tail_f)
            bwin = bwin + jnp.where(use, keep ** step, 0.0)[:, None, None] * got
    inherited = fwin
    ahead = bwin

    inside = (doc_ids[:, None] == doc_ids[None, :]) & (local[None, :] <= local[:, None])
    distance = jnp.maximum(local[:, None] - local[None, :], 0).astype(jnp.float32)
    weight = jnp.where(inside[None], jnp.exp(-slope[:, None, None] * distance[None]), 0.0)
    scores = exact("thd,shd->hts", lq, lk) * weight
    grad_scores = exact("thv,shv->hts", ldo, lv) * weight
    light_out = mixed("hts,shd->thd", scores, lvf)
    light_dq = mixed("hts,shk->thk", grad_scores, lkf)
    light_dk = mixed("hts,thk->shk", grad_scores, lqf)
    light_dv = mixed("hts,thv->shv", scores, ldof)
    light_out = light_out + mixed("thk,hkv->thv", lqf * head_part[:, :, None], inherited)
    light_dq = light_dq + mixed("thv,hkv->thk", ldof * head_part[:, :, None], inherited)
    light_dk = light_dk + mixed("hqo,sho->shq", ahead, lvf) * tail_part[:, :, None]
    light_dv = light_dv + mixed("hqo,shq->sho", ahead, lkf) * tail_part[:, :, None]

    span = len(key_blocks) * rows
    key_all = jnp.concatenate([b for (b, _), _ in key_blocks], axis=0)
    keys = key_all[:, :cols].reshape(span, heads, width)
    values = key_all[:, cols : 2 * cols].reshape(span, heads, width)
    key_ids = jnp.concatenate([i[0] for (_, i), _ in key_blocks])
    key_pos = jnp.concatenate([base * rows + local for _, base in key_blocks])
    allowed = (
        (key_pos[None, :] >= 0)
        & (key_pos[None, :] <= positions[:, None])
        & (key_ids[None, :] == doc_ids[:, None])
    )[None]
    logits = exact("thd,shd->hts", sq, keys) * scale
    masked = jnp.where(allowed, logits, -1e30)
    top = jnp.max(masked, axis=2)
    raw = jnp.where(allowed, jnp.exp(masked - top[:, :, None]), 0.0)
    total = jnp.sum(raw, axis=2)
    accum = exact("hts,shd->htd", raw.astype(jnp.bfloat16), values)
    soft_out = jnp.transpose(accum / total[:, :, None], (1, 0, 2)).astype(jnp.bfloat16)
    lse = top + jnp.log(total)
    delta = jnp.sum(sdo.astype(jnp.float32) * soft_out.astype(jnp.float32), axis=2).T
    prob = jnp.where(allowed, jnp.exp(jnp.where(allowed, logits - lse[:, :, None], -1e30)), 0.0)
    dprob = exact("thd,shd->hts", sdo, values)
    dlogit = (prob * (dprob - delta[:, :, None])).astype(jnp.bfloat16)
    soft_dq = exact("hts,shd->thd", dlogit, keys) * scale

    stats = jnp.stack([lse, delta])
    stat_blocks = [stats, swapped(stats)]
    for rnd in range(1, chip_hops + 1):
        stat_blocks.append(shifted(stats, -2 * rnd))
        stat_blocks.append(crossed(stats, -2 * rnd))
    soft_dq, stat_blocks = lax.optimization_barrier((soft_dq, stat_blocks))
    query_all = jnp.concatenate([b for (b, _), _ in query_blocks], axis=0)
    queries = query_all[:, :cols].reshape(span, heads, width)
    grads = query_all[:, cols : 2 * cols].reshape(span, heads, width)
    query_ids = jnp.concatenate([i[0] for (_, i), _ in query_blocks])
    stat_all = jnp.concatenate(stat_blocks, axis=2)
    lse_all, delta_all = stat_all[0], stat_all[1]
    query_pos = jnp.concatenate([base * rows + local for _, base in query_blocks])
    seen = (
        (query_pos[:, None] < total_rows)
        & (positions[None, :] <= query_pos[:, None])
        & (doc_ids[None, :] == query_ids[:, None])
    )[None]
    logits_t = exact("thd,shd->hts", queries, sk) * scale
    prob_t = jnp.where(seen, jnp.exp(jnp.where(seen, logits_t - lse_all[:, :, None], -1e30)), 0.0)
    soft_dv = exact("hts,thd->shd", prob_t.astype(jnp.bfloat16), grads)
    dprob_t = exact("thd,shd->hts", grads, sv)
    dlogit_t = (prob_t * (dprob_t - delta_all[:, :, None])).astype(jnp.bfloat16)
    soft_dk = exact("hts,thd->shd", dlogit_t, queries) * scale

    flat = (rows, heads * width)
    return (
        light_out.reshape(flat).astype(jnp.bfloat16),
        light_dq.reshape(flat).astype(jnp.bfloat16),
        light_dk.reshape(flat).astype(jnp.bfloat16),
        light_dv.reshape(flat).astype(jnp.bfloat16),
        soft_out.reshape(flat),
        soft_dq.reshape(flat).astype(jnp.bfloat16),
        soft_dk.reshape(flat).astype(jnp.bfloat16),
        soft_dv.reshape(flat).astype(jnp.bfloat16),
    )


def solution(mesh):
    row = P(("dp", "seq"), "head")
    return jax.shard_map(
        per_device,
        mesh=mesh,
        in_specs=(P(("dp", "seq")), row, row, row, P("head"), row, row, row, row, row),
        out_specs=(row,) * 8,
        check_vma=False,
    )
```

```python
import jax
import jax.numpy as jnp
from jax import lax
from jax.sharding import PartitionSpec as P

PRECISE = lax.Precision.HIGH
REACH = 8


def mixed(form, left, right):
    return jnp.einsum(form, left, right, precision=PRECISE, preferred_element_type=jnp.float32)


def exact(form, left, right):
    return jnp.einsum(form, left, right, preferred_element_type=jnp.float32)


def relay(value, steps, shift):
    count = lax.axis_size("seq")
    pairs = [(s, s + shift) for s in range(count) if 0 <= s + shift < count]
    out = []
    cur = value
    for _ in range(steps):
        cur = lax.ppermute(cur, "seq", pairs)
        out.append(cur)
    return out


def shifted(value, shift):
    count = lax.axis_size("seq")
    pairs = [(s, s + shift) for s in range(count) if 0 <= s + shift < count]
    return lax.ppermute(value, "seq", pairs)


def swapped(value):
    count = lax.axis_size("seq")
    return lax.ppermute(value, "seq", [(s, s ^ 1) for s in range(count)])


def crossed(value, shift):
    count = lax.axis_size("seq")
    pairs = [(s, (s + shift) ^ 1) for s in range(count) if 0 <= s + shift < count]
    return lax.ppermute(value, "seq", pairs)


def per_device(
    doc_ids,
    light_q,
    light_k,
    light_v,
    light_decay,
    light_grad_out,
    soft_q,
    soft_k,
    soft_v,
    soft_grad_out,
):
    rows = light_q.shape[0]
    heads = light_decay.shape[0]
    width = light_q.shape[1] // heads
    count = lax.axis_size("seq")
    me = lax.axis_index("seq")
    total_rows = rows * count
    reach = min(REACH, count - 1)
    scale = width ** (-0.5)

    local = jnp.arange(rows, dtype=jnp.int32)
    positions = me * rows + local
    head_id = doc_ids[0]
    tail_id = doc_ids[-1]
    slope = light_decay

    def shape3(a):
        return a.reshape(rows, heads, width)

    lq, lk, lv, ldo = shape3(light_q), shape3(light_k), shape3(light_v), shape3(light_grad_out)
    sq, sk, sv, sdo = shape3(soft_q), shape3(soft_k), shape3(soft_v), shape3(soft_grad_out)
    lqf, lkf, lvf, ldof = (a.astype(jnp.float32) for a in (lq, lk, lv, ldo))
    cols = heads * width
    own_ids = doc_ids[None, :]

    own_kv = (jnp.concatenate([soft_k, soft_v], axis=1), own_ids)
    own_qg = (jnp.concatenate([soft_q, soft_grad_out], axis=1), own_ids)
    partner = me ^ 1

    since_start = (local + 1).astype(jnp.float32)
    until_end = (rows - 1 - local).astype(jnp.float32)
    start_decay = jnp.exp(-since_start[:, None] * slope[None, :])
    end_decay = jnp.exp(-until_end[:, None] * slope[None, :])
    tail_part = end_decay * (doc_ids == tail_id)[:, None]
    head_part = start_decay * (doc_ids == head_id)[:, None]
    send_state = mixed("shk,shv->hkv", lkf * tail_part[:, :, None], lvf)
    back_state = mixed("thq,tho->hqo", lqf * head_part[:, :, None], ldof)
    keep = jnp.exp(-slope * rows)
    head_f = head_id.astype(jnp.float32)
    tail_f = tail_id.astype(jnp.float32)

    def tagged(state, tag_a, tag_b):
        tags = jnp.zeros((heads, 8, width), jnp.float32).at[:, 0, 0].set(tag_a).at[:, 0, 1].set(tag_b)
        return jnp.concatenate([state, tags], axis=1)

    def untag(message):
        return message[:, :width], message[0, width, 0], message[0, width, 1]

    chip_hops = (reach + 1) // 2
    key_blocks = [(own_kv, me)]
    query_blocks = [(own_qg, me)]
    z_kv, z_qg = own_kv, own_qg
    fwin = bwin = None
    light_steps = [1]
    while light_steps[-1] * 2 < reach:
        light_steps.append(light_steps[-1] * 2)
    light_at = {i + 1: st for i, st in enumerate(light_steps[:-1])}
    light_at[chip_hops] = light_steps[-1]
    for rnd in range(chip_hops + 1):
        sent = {}
        if rnd < chip_hops:
            sent["z_kv"] = shifted(z_kv, 2)
            sent["z_qg"] = shifted(z_qg, -2)
        sent["w_kv"] = swapped(z_kv)
        sent["w_qg"] = swapped(z_qg)
        if rnd == 0:
            sent["f"] = shifted(tagged(send_state, head_f, tail_f).astype(jnp.bfloat16), 1)
            sent["b"] = shifted(tagged(back_state, head_f, tail_f).astype(jnp.bfloat16), -1)
        elif rnd in light_at:
            step = light_at[rnd]
            sent["f"] = shifted(tagged(fwin, head_f, tail_f).astype(jnp.bfloat16), step)
            sent["b"] = shifted(tagged(bwin, head_f, tail_f).astype(jnp.bfloat16), -step)
        sent = lax.optimization_barrier(sent)
        key_blocks.append((sent["w_kv"], partner - 2 * rnd))
        query_blocks.append((sent["w_qg"], partner + 2 * rnd))
        if rnd < chip_hops:
            z_kv, z_qg = sent["z_kv"], sent["z_qg"]
            key_blocks.append((z_kv, me - 2 * (rnd + 1)))
            query_blocks.append((z_qg, me + 2 * (rnd + 1)))
        if rnd == 0:
            got, _, src_tail = untag(sent["f"].astype(jnp.float32))
            fwin = jnp.where((me >= 1) & (src_tail == head_f), 1.0, 0.0) * got
            got, src_head, _ = untag(sent["b"].astype(jnp.float32))
            bwin = jnp.where((me + 1 < count) & (src_head == tail_f), 1.0, 0.0) * got
        elif rnd in light_at:
            step = light_at[rnd]
            got, src_head, _ = untag(sent["f"].astype(jnp.float32))
            use = (me >= step) & (src_head == head_f)
            fwin = fwin + jnp.where(use, keep ** step, 0.0)[:, None, None] * got
            got, _, src_tail = untag(sent["b"].astype(jnp.float32))
            use = (me + step < count) & (src_tail == tail_f)
            bwin = bwin + jnp.where(use, keep ** step, 0.0)[:, None, None] * got
    inherited = fwin
    ahead = bwin

    inside = (doc_ids[:, None] == doc_ids[None, :]) & (local[None, :] <= local[:, None])
    distance = jnp.maximum(local[:, None] - local[None, :], 0).astype(jnp.float32)
    weight = jnp.where(inside[None], jnp.exp(-slope[:, None, None] * distance[None]), 0.0)
    scores = exact("thd,shd->hts", lq, lk) * weight
    grad_scores = exact("thv,shv->hts", ldo, lv) * weight
    light_out = mixed("hts,shd->thd", scores, lvf)
    light_dq = mixed("hts,shk->thk", grad_scores, lkf)
    light_dk = mixed("hts,thk->shk", grad_scores, lqf)
    light_dv = mixed("hts,thv->shv", scores, ldof)
    light_out = light_out + mixed("thk,hkv->thv", lqf * head_part[:, :, None], inherited)
    light_dq = light_dq + mixed("thv,hkv->thk", ldof * head_part[:, :, None], inherited)
    light_dk = light_dk + mixed("hqo,sho->shq", ahead, lvf) * tail_part[:, :, None]
    light_dv = light_dv + mixed("hqo,shq->sho", ahead, lkf) * tail_part[:, :, None]

    span = len(key_blocks) * rows
    key_all = jnp.concatenate([b for (b, _), _ in key_blocks], axis=0)
    keys = key_all[:, :cols].reshape(span, heads, width)
    values = key_all[:, cols : 2 * cols].reshape(span, heads, width)
    key_ids = jnp.concatenate([i[0] for (_, i), _ in key_blocks])
    key_pos = jnp.concatenate([base * rows + local for _, base in key_blocks])
    allowed = (
        (key_pos[None, :] >= 0)
        & (key_pos[None, :] <= positions[:, None])
        & (key_ids[None, :] == doc_ids[:, None])
    )[None]
    logits = exact("thd,shd->hts", sq, keys) * scale
    masked = jnp.where(allowed, logits, -1e30)
    top = jnp.max(masked, axis=2)
    raw = jnp.where(allowed, jnp.exp(masked - top[:, :, None]), 0.0)
    total = jnp.sum(raw, axis=2)
    accum = exact("hts,shd->htd", raw.astype(jnp.bfloat16), values)
    soft_out = jnp.transpose(accum / total[:, :, None], (1, 0, 2)).astype(jnp.bfloat16)
    lse = top + jnp.log(total)
    delta = jnp.sum(sdo.astype(jnp.float32) * soft_out.astype(jnp.float32), axis=2).T
    prob = jnp.where(allowed, jnp.exp(jnp.where(allowed, logits - lse[:, :, None], -1e30)), 0.0)
    dprob = exact("thd,shd->hts", sdo, values)
    dlogit = (prob * (dprob - delta[:, :, None])).astype(jnp.bfloat16)
    soft_dq = exact("hts,shd->thd", dlogit, keys) * scale

    stats = jnp.stack([lse, delta])
    stat_blocks = [stats, swapped(stats)]
    for rnd in range(1, chip_hops + 1):
        stat_blocks.append(shifted(stats, -2 * rnd))
        stat_blocks.append(crossed(stats, -2 * rnd))
    soft_dq, stat_blocks = lax.optimization_barrier((soft_dq, stat_blocks))
    query_all = jnp.concatenate([b for (b, _), _ in query_blocks], axis=0)
    queries = query_all[:, :cols].reshape(span, heads, width)
    grads = query_all[:, cols : 2 * cols].reshape(span, heads, width)
    query_ids = jnp.concatenate([i[0] for (_, i), _ in query_blocks])
    stat_all = jnp.concatenate(stat_blocks, axis=2)
    lse_all, delta_all = stat_all[0], stat_all[1]
    query_pos = jnp.concatenate([base * rows + local for _, base in query_blocks])
    seen = (
        (query_pos[:, None] < total_rows)
        & (positions[None, :] <= query_pos[:, None])
        & (doc_ids[None, :] == query_ids[:, None])
    )[None]
    logits_t = exact("thd,shd->hts", queries, sk) * scale
    prob_t = jnp.where(seen, jnp.exp(jnp.where(seen, logits_t - lse_all[:, :, None], -1e30)), 0.0)
    soft_dv = exact("hts,thd->shd", prob_t.astype(jnp.bfloat16), grads)
    dprob_t = exact("thd,shd->hts", grads, sv)
    dlogit_t = (prob_t * (dprob_t - delta_all[:, :, None])).astype(jnp.bfloat16)
    soft_dk = exact("hts,thd->shd", dlogit_t, queries) * scale

    flat = (rows, heads * width)
    return (
        light_out.reshape(flat).astype(jnp.bfloat16),
        light_dq.reshape(flat).astype(jnp.bfloat16),
        light_dk.reshape(flat).astype(jnp.bfloat16),
        light_dv.reshape(flat).astype(jnp.bfloat16),
        soft_out.reshape(flat),
        soft_dq.reshape(flat).astype(jnp.bfloat16),
        soft_dk.reshape(flat).astype(jnp.bfloat16),
        soft_dv.reshape(flat).astype(jnp.bfloat16),
    )


def solution(mesh):
    row = P(("dp", "seq"), "head")
    return jax.shard_map(
        per_device,
        mesh=mesh,
        in_specs=(P(("dp", "seq")), row, row, row, P("head"), row, row, row, row, row),
        out_specs=(row,) * 8,
        check_vma=False,
    )
```

```python
import jax
import jax.numpy as jnp
from jax import lax
from jax.sharding import PartitionSpec as P

PRECISE = lax.Precision.HIGH
REACH = 8


def mixed(form, left, right):
    return jnp.einsum(form, left, right, precision=PRECISE, preferred_element_type=jnp.float32)


def exact(form, left, right):
    return jnp.einsum(form, left, right, preferred_element_type=jnp.float32)


def relay(value, steps, shift):
    count = lax.axis_size("seq")
    pairs = [(s, s + shift) for s in range(count) if 0 <= s + shift < count]
    out = []
    cur = value
    for _ in range(steps):
        cur = lax.ppermute(cur, "seq", pairs)
        out.append(cur)
    return out


def shifted(value, shift):
    count = lax.axis_size("seq")
    pairs = [(s, s + shift) for s in range(count) if 0 <= s + shift < count]
    return lax.ppermute(value, "seq", pairs)


def swapped(value):
    count = lax.axis_size("seq")
    return lax.ppermute(value, "seq", [(s, s ^ 1) for s in range(count)])


def crossed(value, shift):
    count = lax.axis_size("seq")
    pairs = [(s, (s + shift) ^ 1) for s in range(count) if 0 <= s + shift < count]
    return lax.ppermute(value, "seq", pairs)


def per_device(
    doc_ids,
    light_q,
    light_k,
    light_v,
    light_decay,
    light_grad_out,
    soft_q,
    soft_k,
    soft_v,
    soft_grad_out,
):
    rows = light_q.shape[0]
    heads = light_decay.shape[0]
    width = light_q.shape[1] // heads
    count = lax.axis_size("seq")
    me = lax.axis_index("seq")
    total_rows = rows * count
    reach = min(REACH, count - 1)
    scale = width ** (-0.5)

    local = jnp.arange(rows, dtype=jnp.int32)
    positions = me * rows + local
    head_id = doc_ids[0]
    tail_id = doc_ids[-1]
    slope = light_decay

    def shape3(a):
        return a.reshape(rows, heads, width)

    lq, lk, lv, ldo = shape3(light_q), shape3(light_k), shape3(light_v), shape3(light_grad_out)
    sq, sk, sv, sdo = shape3(soft_q), shape3(soft_k), shape3(soft_v), shape3(soft_grad_out)
    lqf, lkf, lvf, ldof = (a.astype(jnp.float32) for a in (lq, lk, lv, ldo))
    cols = heads * width
    own_ids = doc_ids[None, :]

    own_kv = (jnp.concatenate([soft_k, soft_v], axis=1), own_ids)
    own_qg = (jnp.concatenate([soft_q, soft_grad_out], axis=1), own_ids)
    partner = me ^ 1

    since_start = (local + 1).astype(jnp.float32)
    until_end = (rows - 1 - local).astype(jnp.float32)
    start_decay = jnp.exp(-since_start[:, None] * slope[None, :])
    end_decay = jnp.exp(-until_end[:, None] * slope[None, :])
    tail_part = end_decay * (doc_ids == tail_id)[:, None]
    head_part = start_decay * (doc_ids == head_id)[:, None]
    send_state = mixed("shk,shv->hkv", lkf * tail_part[:, :, None], lvf)
    back_state = mixed("thq,tho->hqo", lqf * head_part[:, :, None], ldof)
    keep = jnp.exp(-slope * rows)
    head_f = head_id.astype(jnp.float32)
    tail_f = tail_id.astype(jnp.float32)

    def tagged(state, tag_a, tag_b):
        tags = jnp.zeros((heads, 8, width), jnp.float32).at[:, 0, 0].set(tag_a).at[:, 0, 1].set(tag_b)
        return jnp.concatenate([state, tags], axis=1)

    def untag(message):
        return message[:, :width], message[0, width, 0], message[0, width, 1]

    chip_hops = (reach + 1) // 2
    key_blocks = [(own_kv, me)]
    query_blocks = [(own_qg, me)]
    z_kv, z_qg = own_kv, own_qg
    fwin = bwin = None
    light_steps = [1]
    while light_steps[-1] * 2 < reach:
        light_steps.append(light_steps[-1] * 2)
    light_at = {i + 1: st for i, st in enumerate(light_steps[:-1])}
    light_at[chip_hops] = light_steps[-1]
    for rnd in range(chip_hops + 1):
        sent = {}
        if rnd < chip_hops:
            sent["z_kv"] = shifted(z_kv, 2)
            sent["z_qg"] = shifted(z_qg, -2)
        sent["w_kv"] = swapped(z_kv)
        sent["w_qg"] = swapped(z_qg)
        if rnd == 0:
            sent["f"] = shifted(tagged(send_state, head_f, tail_f).astype(jnp.bfloat16), 1)
            sent["b"] = shifted(tagged(back_state, head_f, tail_f).astype(jnp.bfloat16), -1)
        elif rnd in light_at:
            step = light_at[rnd]
            sent["f"] = shifted(tagged(fwin, head_f, tail_f).astype(jnp.bfloat16), step)
            sent["b"] = shifted(tagged(bwin, head_f, tail_f).astype(jnp.bfloat16), -step)
        if rnd < chip_hops:
            sent = lax.optimization_barrier(sent)
        key_blocks.append((sent["w_kv"], partner - 2 * rnd))
        query_blocks.append((sent["w_qg"], partner + 2 * rnd))
        if rnd < chip_hops:
            z_kv, z_qg = sent["z_kv"], sent["z_qg"]
            key_blocks.append((z_kv, me - 2 * (rnd + 1)))
            query_blocks.append((z_qg, me + 2 * (rnd + 1)))
        if rnd == 0:
            got, _, src_tail = untag(sent["f"].astype(jnp.float32))
            fwin = jnp.where((me >= 1) & (src_tail == head_f), 1.0, 0.0) * got
            got, src_head, _ = untag(sent["b"].astype(jnp.float32))
            bwin = jnp.where((me + 1 < count) & (src_head == tail_f), 1.0, 0.0) * got
        elif rnd in light_at:
            step = light_at[rnd]
            got, src_head, _ = untag(sent["f"].astype(jnp.float32))
            use = (me >= step) & (src_head == head_f)
            fwin = fwin + jnp.where(use, keep ** step, 0.0)[:, None, None] * got
            got, _, src_tail = untag(sent["b"].astype(jnp.float32))
            use = (me + step < count) & (src_tail == tail_f)
            bwin = bwin + jnp.where(use, keep ** step, 0.0)[:, None, None] * got
    inherited = fwin
    ahead = bwin

    inside = (doc_ids[:, None] == doc_ids[None, :]) & (local[None, :] <= local[:, None])
    distance = jnp.maximum(local[:, None] - local[None, :], 0).astype(jnp.float32)
    weight = jnp.where(inside[None], jnp.exp(-slope[:, None, None] * distance[None]), 0.0)
    scores = exact("thd,shd->hts", lq, lk) * weight
    grad_scores = exact("thv,shv->hts", ldo, lv) * weight
    light_out = mixed("hts,shd->thd", scores, lvf)
    light_dq = mixed("hts,shk->thk", grad_scores, lkf)
    light_dk = mixed("hts,thk->shk", grad_scores, lqf)
    light_dv = mixed("hts,thv->shv", scores, ldof)
    light_out = light_out + mixed("thk,hkv->thv", lqf * head_part[:, :, None], inherited)
    light_dq = light_dq + mixed("thv,hkv->thk", ldof * head_part[:, :, None], inherited)
    light_dk = light_dk + mixed("hqo,sho->shq", ahead, lvf) * tail_part[:, :, None]
    light_dv = light_dv + mixed("hqo,shq->sho", ahead, lkf) * tail_part[:, :, None]

    span = len(key_blocks) * rows
    key_all = jnp.concatenate([b for (b, _), _ in key_blocks], axis=0)
    keys = key_all[:, :cols].reshape(span, heads, width)
    values = key_all[:, cols : 2 * cols].reshape(span, heads, width)
    key_ids = jnp.concatenate([i[0] for (_, i), _ in key_blocks])
    key_pos = jnp.concatenate([base * rows + local for _, base in key_blocks])
    allowed = (
        (key_pos[None, :] >= 0)
        & (key_pos[None, :] <= positions[:, None])
        & (key_ids[None, :] == doc_ids[:, None])
    )[None]
    logits = exact("thd,shd->hts", sq, keys) * scale
    masked = jnp.where(allowed, logits, -1e30)
    top = jnp.max(masked, axis=2)
    raw = jnp.where(allowed, jnp.exp(masked - top[:, :, None]), 0.0)
    total = jnp.sum(raw, axis=2)
    accum = exact("hts,shd->htd", raw.astype(jnp.bfloat16), values)
    soft_out = jnp.transpose(accum / total[:, :, None], (1, 0, 2)).astype(jnp.bfloat16)
    lse = top + jnp.log(total)
    delta = jnp.sum(sdo.astype(jnp.float32) * soft_out.astype(jnp.float32), axis=2).T
    prob = jnp.where(allowed, jnp.exp(jnp.where(allowed, logits - lse[:, :, None], -1e30)), 0.0)
    dprob = exact("thd,shd->hts", sdo, values)
    dlogit = (prob * (dprob - delta[:, :, None])).astype(jnp.bfloat16)
    soft_dq = exact("hts,shd->thd", dlogit, keys) * scale

    stats = jnp.stack([lse, delta])
    stat_blocks = [stats, swapped(stats)]
    for rnd in range(1, chip_hops + 1):
        stat_blocks.append(shifted(stats, -2 * rnd))
        stat_blocks.append(crossed(stats, -2 * rnd))
    soft_dq, stat_blocks = lax.optimization_barrier((soft_dq, stat_blocks))
    query_all = jnp.concatenate([b for (b, _), _ in query_blocks], axis=0)
    queries = query_all[:, :cols].reshape(span, heads, width)
    grads = query_all[:, cols : 2 * cols].reshape(span, heads, width)
    query_ids = jnp.concatenate([i[0] for (_, i), _ in query_blocks])
    stat_all = jnp.concatenate(stat_blocks, axis=2)
    lse_all, delta_all = stat_all[0], stat_all[1]
    query_pos = jnp.concatenate([base * rows + local for _, base in query_blocks])
    seen = (
        (query_pos[:, None] < total_rows)
        & (positions[None, :] <= query_pos[:, None])
        & (doc_ids[None, :] == query_ids[:, None])
    )[None]
    logits_t = exact("thd,shd->hts", queries, sk) * scale
    prob_t = jnp.where(seen, jnp.exp(jnp.where(seen, logits_t - lse_all[:, :, None], -1e30)), 0.0)
    soft_dv = exact("hts,thd->shd", prob_t.astype(jnp.bfloat16), grads)
    dprob_t = exact("thd,shd->hts", grads, sv)
    dlogit_t = (prob_t * (dprob_t - delta_all[:, :, None])).astype(jnp.bfloat16)
    soft_dk = exact("hts,thd->shd", dlogit_t, queries) * scale

    flat = (rows, heads * width)
    return (
        light_out.reshape(flat).astype(jnp.bfloat16),
        light_dq.reshape(flat).astype(jnp.bfloat16),
        light_dk.reshape(flat).astype(jnp.bfloat16),
        light_dv.reshape(flat).astype(jnp.bfloat16),
        soft_out.reshape(flat),
        soft_dq.reshape(flat).astype(jnp.bfloat16),
        soft_dk.reshape(flat).astype(jnp.bfloat16),
        soft_dv.reshape(flat).astype(jnp.bfloat16),
    )


def solution(mesh):
    row = P(("dp", "seq"), "head")
    return jax.shard_map(
        per_device,
        mesh=mesh,
        in_specs=(P(("dp", "seq")), row, row, row, P("head"), row, row, row, row, row),
        out_specs=(row,) * 8,
        check_vma=False,
    )
```
